32 devices in a mesh: grp: 2 (over x), ha: 16 (over z, y, core).
Axes of the slice: x: 2, y: 2, z: 4, core: 2. Of those that a mesh axis runs over, the one named last changes fastest.
Arguments:
- features: bfloat16 [4, 16, 128, 384], P('grp', 'ha'), parts along dimension 0, may hold values from -8 to 8
- first_cache: bfloat16 [4, 16, 128, 384], P('grp', 'ha'), parts along dimension 0, may hold values from -6 to 6
- second_cache: bfloat16 [4, 32, 256, 192], P('grp', 'ha'), parts along dimension 0, may hold values from -6 to 6
- w_query: bfloat16 [384, 384], replicated, may hold values from -2 to 2
- w_key: bfloat16 [384, 384], replicated, may hold values from -2 to 2
- w_value: bfloat16 [384, 384], replicated, may hold values from -0.3125 to 0.3125
- w_output: bfloat16 [384, 384], replicated, may hold values from -0.625 to 0.625
- w_first: bfloat16 [3, 3, 3, 384, 384], replicated, may hold values from -0.0625 to 0.0625
- w_upsample: bfloat16 [3, 3, 384, 192], replicated, may hold values from -0.109375 to 0.109375
- w_second: bfloat16 [3, 3, 3, 192, 192], replicated, may hold values from -0.078125 to 0.078125
Outputs:
- decoded: bfloat16 [4, 32, 256, 192], P('grp', 'ha'), parts along dimension 0
The draws below stay inside these ranges and needn't reach their ends.
There are 2 independent parts, one for each index of `grp`. The reference program is written for one: setup_inputs(seed, part) draws one part's arguments, and reference() takes and returns one part's arrays. A program takes and returns all parts, laid end to end along the dimension named above; an argument that names none is the same for every part. Nothing has to cross between parts.
All inputs are finite; a program needn't handle non-finite values.
Results may differ from the reference program's by a relative error of at most 0.015.
Values may be sent and summed in bfloat16 or wider, within the bound.
No kernel may reach another device: no remote copies, remote signals or barrier semaphores. Data moves between devices by JAX's collectives and lax.ppermute only.
A program may use at most 128 MiB of HBM per device.

```python
import math
import jax
import jax.numpy as jnp
from jax import lax

C = 384
C2 = 192
CACHE_T = 2
FRAMES = 2
LAT_W = 128
LAT_H = 16


def query_key_pair(key):
    base = jnp.clip(jax.random.normal(jax.random.fold_in(key, 101), (C, C), jnp.float32), -4.0, 4.0)
    other = jnp.clip(jax.random.normal(jax.random.fold_in(key, 102), (C, C), jnp.float32), -4.0, 4.0)
    spread = math.sqrt(math.log(LAT_H * LAT_W / 8.0))
    sigma = math.sqrt(spread / C)
    first = base * sigma
    second = other * sigma
    return (first, second)


def draw_w_query(key, part):
    return query_key_pair(key)[0].astype(jnp.bfloat16)


def draw_w_key(key, part):
    return query_key_pair(key)[1].astype(jnp.bfloat16)


def draw_features(key, part):
    shape = (FRAMES, LAT_H, LAT_W, C)
    result = jnp.clip(jax.random.normal(jax.random.fold_in(key, 206), shape, jnp.float32), -6.0, 6.0)
    return result.astype(jnp.bfloat16)


def level_of(key, dims, cuts, smallest, top_value):
    def one(position, shards_of):
        steps = jax.random.uniform(jax.random.fold_in(jax.random.fold_in(key, 6), position), (shards_of,), jnp.float32, smallest / len(cuts), top_value / len(cuts))
        return jnp.repeat(jnp.exp(steps), dims[position] // shards_of).reshape((-1,) + (1,) * (len(dims) - position - 1))

    level = one(*cuts[0])
    for cut in cuts[1:]:
        level = level * one(*cut)
    return level


def gaussian(stream_key, dims, scale, limit, pieces=(), kind=jnp.bfloat16):
    level = level_of(stream_key, dims, pieces, -0.22, 0.18) if pieces else 1.0
    values = jax.random.normal(stream_key, dims, jnp.float32) * scale * level
    return jnp.minimum(jnp.maximum(values, -limit), limit).astype(kind)


def setup_inputs(seed: int = 0, part: int = 0) -> dict:
    key_list = jax.random.split(jax.random.key(seed), 11)
    own_keys = jax.random.split(jax.random.fold_in(key_list[10], part), 11)
    features = draw_features(jax.random.fold_in(jax.random.fold_in(key_list[10], part), 71), part)
    first_cache = gaussian(own_keys[1], (CACHE_T, LAT_H, LAT_W, C), 1.0, 6.0, ((1, 16),))
    second_cache = gaussian(own_keys[2], (CACHE_T, 2 * LAT_H, 2 * LAT_W, C2), 1.0, 6.0, ((1, 16),))
    w_query = draw_w_query(jax.random.fold_in(key_list[10], 71), part)
    w_key = draw_w_key(jax.random.fold_in(key_list[10], 71), part)
    w_value = gaussian(key_list[5], (C, C), C ** -0.5, 0.3125)
    w_output = gaussian(key_list[6], (C, C), (C // 4) ** -0.5, 0.625)
    w_first = gaussian(key_list[7], (3, 3, 3, C, C), (27 * C) ** -0.5, 0.0625)
    w_upsample = gaussian(key_list[8], (3, 3, C, C2), (9 * C) ** -0.5, 0.109375)
    w_second = gaussian(key_list[9], (3, 3, 3, C2, C2), (27 * C2) ** -0.5, 0.078125)
    return dict(features=features, first_cache=first_cache, second_cache=second_cache, w_query=w_query, w_key=w_key, w_value=w_value, w_output=w_output, w_first=w_first, w_upsample=w_upsample, w_second=w_second)


def rms_scale(tensor):
    widened = tensor.astype(jnp.float32)
    return widened * lax.rsqrt(lax.optimization_barrier(jnp.mean(widened * widened, axis=-1, keepdims=True)) + 1e-06)

def conv_apply(stacked, weight, time_taps):
    padded = jnp.pad(stacked.astype(jnp.float32), ((0, 0), (1, 1), (1, 1), (0, 0)))
    frames_out = stacked.shape[0] - time_taps + 1
    height_out = stacked.shape[1]
    width_out = stacked.shape[2]
    result = jnp.zeros((frames_out, height_out, width_out, weight.shape[-1]), jnp.float32)
    for time_off in range(time_taps):
        for row_off in range(3):
            for col_off in range(3):
                window = padded[time_off:time_off + frames_out, row_off:row_off + height_out, col_off:col_off + width_out]
                kernel = weight[time_off, row_off, col_off].astype(jnp.float32)
                result = result + jnp.einsum('fhwc,cd->fhwd', window, kernel)
    return result

def attend_frame(queries, keys_all, values_all):
    token_count = queries.shape[0]
    block = math.gcd(token_count, 512)
    score_scale = 1.0 / math.sqrt(queries.shape[1])

    def one_block(query_rows):
        scores = jnp.dot(query_rows, keys_all.T, preferred_element_type=jnp.float32) * score_scale
        largest = lax.optimization_barrier(jnp.max(scores, axis=-1, keepdims=True))
        weights = jnp.exp(scores - largest)
        weight_sum = lax.optimization_barrier(jnp.sum(weights, axis=-1, keepdims=True))
        summed = jnp.dot(weights.astype(jnp.bfloat16), values_all, preferred_element_type=jnp.float32)
        return (summed / weight_sum).astype(jnp.bfloat16)
    blocks = queries.reshape(token_count // block, block, queries.shape[1])
    return lax.map(one_block, blocks).reshape(token_count, queries.shape[1])

def reference(features, first_cache, second_cache, w_query, w_key, w_value, w_output, w_first, w_upsample, w_second):
    frame_count, height, width, channels = features.shape
    normed = rms_scale(features).astype(jnp.bfloat16)
    mixed_frames = []
    for frame in range(frame_count):
        tokens = normed[frame].reshape(height * width, channels)
        queries = jnp.dot(tokens, w_query, preferred_element_type=jnp.float32).astype(jnp.bfloat16)
        keys_all = jnp.dot(tokens, w_key, preferred_element_type=jnp.float32).astype(jnp.bfloat16)
        values_all = jnp.dot(tokens, w_value, preferred_element_type=jnp.float32).astype(jnp.bfloat16)
        attended = attend_frame(queries, keys_all, values_all)
        projected = jnp.dot(attended, w_output, preferred_element_type=jnp.float32)
        mixed_frames.append((features[frame].astype(jnp.float32) + projected.reshape(height, width, channels)).astype(jnp.bfloat16))
    mixed = jnp.stack(mixed_frames, axis=0)
    first_in = jax.nn.silu(rms_scale(mixed)).astype(jnp.bfloat16)
    first_stack = jnp.concatenate([first_cache, first_in], axis=0)
    block_out = (mixed.astype(jnp.float32) + conv_apply(first_stack, w_first, 3)).astype(jnp.bfloat16)
    enlarged = jnp.repeat(jnp.repeat(block_out, 2, axis=1), 2, axis=2)
    upsampled = conv_apply(enlarged, w_upsample[None], 1).astype(jnp.bfloat16)
    second_in = jax.nn.silu(rms_scale(upsampled)).astype(jnp.bfloat16)
    second_stack = jnp.concatenate([second_cache, second_in], axis=0)
    return (upsampled.astype(jnp.float32) + conv_apply(second_stack, w_second, 3)).astype(jnp.bfloat16)
```

```python
import math

import jax
import jax.numpy as jnp
from jax import lax
from jax.sharding import PartitionSpec as P


def halo_rows(x, dim, width):
    count, length = (lax.axis_size("ha"), x.shape[dim])
    up = [(i, i + 1) for i in range(count - 1)]
    down = [(j, i) for i, j in up]
    last = lax.slice_in_dim(x, length - width, length, axis=dim)
    first = lax.slice_in_dim(x, 0, width, axis=dim)
    before = lax.ppermute(last, "ha", up)
    after = lax.ppermute(first, "ha", down)
    return before, after


def extended(x, dim, width):
    before, after = halo_rows(x, dim, width)
    return jnp.concatenate([before, x, after], axis=dim)


def gather_rows(x):
    count = lax.axis_size("ha")
    chips = count // 2
    pieces = [x]
    for shift in range(1, chips):
        pairs = [
            (2 * c + k, 2 * ((c + shift) % chips) + k) for c in range(chips) for k in range(2)
        ]
        pieces.append(lax.ppermute(x, "ha", pairs))
    own_chip = jnp.concatenate(pieces, axis=1)
    swap = [(2 * c + k, 2 * c + 1 - k) for c in range(chips) for k in range(2)]
    other = lax.ppermute(own_chip, "ha", swap)
    return jnp.concatenate([own_chip, other], axis=1)


def rms_scale(tensor):
    widened = tensor.astype(jnp.float32)
    return widened * lax.rsqrt(jnp.mean(widened * widened, axis=-1, keepdims=True) + 1e-06)


def conv_taps(padded, weight, time_taps):
    frames_out = padded.shape[0] - time_taps + 1
    height_out = padded.shape[1] - 2
    width_out = padded.shape[2]
    in_channels = weight.shape[-2]
    out_channels = weight.shape[-1]
    widened = jnp.pad(padded, ((0, 0), (0, 0), (1, 1), (0, 0)))
    result = jnp.zeros((frames_out, height_out, width_out, out_channels), jnp.float32)
    for time_off in range(time_taps):
        for row_off in range(3):
            window = widened[time_off : time_off + frames_out, row_off : row_off + height_out]
            stacked = jnp.concatenate(
                [window[:, :, col_off : col_off + width_out] for col_off in range(3)], axis=-1
            )
            kernel = weight[time_off, row_off].reshape(3 * in_channels, out_channels)
            result = result + jnp.einsum(
                "fhwc,cd->fhwd", stacked, kernel, preferred_element_type=jnp.float32
            )
    return result


def project_rows(tokens, weight):
    return jnp.einsum("ftc,cd->ftd", tokens, weight, preferred_element_type=jnp.float32).astype(
        jnp.bfloat16
    )


def per_device(
    features,
    first_cache,
    second_cache,
    w_query,
    w_key,
    w_value,
    w_output,
    w_first,
    w_upsample,
    w_second,
):
    frame_count, row_count, width_count, channels = features.shape
    every_row = gather_rows(features)
    normed_all = rms_scale(every_row).astype(jnp.bfloat16)
    all_tokens = normed_all.reshape(frame_count, -1, channels)
    normed = rms_scale(features).astype(jnp.bfloat16)
    normed_tokens = normed.reshape(frame_count, row_count * width_count, channels)
    queries = project_rows(normed_tokens, w_query)
    keys_all = project_rows(all_tokens, w_key)
    values_all = project_rows(all_tokens, w_value)
    score_scale = 1.0 / math.sqrt(channels)
    scores = (
        jnp.einsum("fqc,fkc->fqk", queries, keys_all, preferred_element_type=jnp.float32)
        * score_scale
    )
    largest = jnp.max(scores, axis=-1)
    weights = jnp.exp(scores - largest[..., None])
    weight_sum = jnp.sum(weights, axis=-1)
    weighted = jnp.einsum(
        "fqk,fkc->fqc",
        weights.astype(jnp.bfloat16),
        values_all,
        preferred_element_type=jnp.float32,
    )
    attended = (weighted / weight_sum[..., None]).astype(jnp.bfloat16)
    projected = jnp.einsum("ftc,cd->ftd", attended, w_output, preferred_element_type=jnp.float32)
    mixed = (
        features.astype(jnp.float32)
        + projected.reshape(frame_count, row_count, width_count, channels)
    ).astype(jnp.bfloat16)
    first_in = jax.nn.silu(rms_scale(mixed)).astype(jnp.bfloat16)
    first_stack = jnp.concatenate([first_cache, first_in], axis=0)
    first_padded = extended(first_stack, 1, 1)
    block_out = (mixed.astype(jnp.float32) + conv_taps(first_padded, w_first, 3)).astype(
        jnp.bfloat16
    )
    block_padded = extended(block_out, 1, 1)
    enlarged = jnp.repeat(jnp.repeat(block_padded, 2, axis=1), 2, axis=2)
    up_padded = enlarged[:, 1 : enlarged.shape[1] - 1]
    upsampled = conv_taps(up_padded, w_upsample[None], 1).astype(jnp.bfloat16)
    second_in = jax.nn.silu(rms_scale(upsampled)).astype(jnp.bfloat16)
    second_stack = jnp.concatenate([second_cache, second_in], axis=0)
    second_padded = extended(second_stack, 1, 1)
    return (upsampled.astype(jnp.float32) + conv_taps(second_padded, w_second, 3)).astype(
        jnp.bfloat16
    )


def solution(mesh):
    placed = (
        P("grp", "ha", None, None),
        P("grp", "ha", None, None),
        P("grp", "ha", None, None),
        P(),
        P(),
        P(),
        P(),
        P(),
        P(),
        P(),
    )
    return jax.shard_map(
        per_device,
        mesh=mesh,
        in_specs=placed,
        out_specs=P("grp", "ha", None, None),
        check_vma=False,
    )
```

```python
import math

import jax
import jax.numpy as jnp
from jax import lax
from jax.sharding import PartitionSpec as P


def halo_rows(x, width):
    count, length = (lax.axis_size("ha"), x.shape[1])
    up = [(i, i + 1) for i in range(count - 1)]
    down = [(j, i) for i, j in up]
    last = lax.slice_in_dim(x, length - width, length, axis=1)
    first = lax.slice_in_dim(x, 0, width, axis=1)
    before = lax.ppermute(last, "ha", up)
    after = lax.ppermute(first, "ha", down)
    return jnp.concatenate([before, x, after], axis=1)


def gather_rows(x):
    count = lax.axis_size("ha")
    chips = count // 2
    pieces = [x]
    for shift in range(1, chips):
        pairs = [
            (2 * c + k, 2 * ((c + shift) % chips) + k) for c in range(chips) for k in range(2)
        ]
        pieces.append(lax.ppermute(x, "ha", pairs))
    own_chip = jnp.concatenate(pieces, axis=1)
    swap = [(2 * c + k, 2 * c + 1 - k) for c in range(chips) for k in range(2)]
    other = lax.ppermute(own_chip, "ha", swap)
    return jnp.concatenate([own_chip, other], axis=1)


def rms_scale(tensor):
    widened = tensor.astype(jnp.float32)
    return widened * lax.rsqrt(jnp.mean(widened * widened, axis=-1, keepdims=True) + 1e-06)


def conv_frames(padded, weight, starts=((0, 1, 2),) * 3, rows=None):
    frames, height, width, channels = padded.shape
    out_rows = height - 2
    cols = jnp.pad(padded, ((0, 0), (0, 0), (1, 1), (0, 0)))
    result = None
    for row_off in range(3):
        if rows is None:
            window = cols[:, row_off : row_off + out_rows]
        else:
            window = jnp.stack([cols[:, r] for r in rows[row_off]], axis=1)
        stacked = jnp.concatenate(
            [window[:, :, s : s + width] for s in starts[row_off]], axis=-1
        )
        kernel = weight[row_off].reshape(3 * channels, weight.shape[-1])
        term = jnp.einsum("fhwc,cd->fhwd", stacked, kernel, preferred_element_type=jnp.float32)
        result = term if result is None else result + term
    return result


def causal_parts(cache_pad, new_pad, weight):
    zero = None
    from_cache = conv_frames(cache_pad, weight[0])
    late = conv_frames(cache_pad[1:2], weight[1])
    zero = jnp.zeros_like(late)
    from_cache = from_cache + jnp.concatenate([late, zero], axis=0)

    def from_new(pad):
        early = conv_frames(pad[0:1], weight[1])
        return conv_frames(pad, weight[2]) + jnp.concatenate([zero, early], axis=0)

    return from_cache, from_new


def project_rows(tokens, weight):
    return jnp.einsum("ftc,cd->ftd", tokens, weight, preferred_element_type=jnp.float32).astype(
        jnp.bfloat16
    )


def upsample_conv(block_pad, weight):
    rows = ((0, 0, 1, 1), (0, 1, 1, 2), (1, 1, 2, 2))
    even = conv_frames(block_pad, weight, starts=((0, 1, 1),) * 3, rows=rows)
    odd = conv_frames(block_pad, weight, starts=((1, 1, 2),) * 3, rows=rows)
    frames, height, width, channels = even.shape
    both = jnp.stack([even, odd], axis=3)
    return both.reshape(frames, height, 2 * width, channels)


def per_device(
    features,
    first_cache,
    second_cache,
    w_query,
    w_key,
    w_value,
    w_output,
    w_first,
    w_upsample,
    w_second,
):
    frame_count, row_count, width_count, channels = features.shape
    me = lax.axis_index("ha")
    count = lax.axis_size("ha")

    first_cache_pad = halo_rows(first_cache, 1)
    second_cache_pad = halo_rows(second_cache, 1)
    first_cached, first_new = causal_parts(first_cache_pad, None, w_first)
    second_cached, second_new = causal_parts(second_cache_pad, None, w_second)

    every_row = gather_rows(features)
    normed_all = rms_scale(every_row).astype(jnp.bfloat16)
    all_tokens = normed_all.reshape(frame_count, -1, channels)
    normed = rms_scale(features).astype(jnp.bfloat16)
    normed_tokens = normed.reshape(frame_count, row_count * width_count, channels)
    queries = project_rows(normed_tokens, w_query)
    keys_all = project_rows(all_tokens, w_key)
    values_all = project_rows(all_tokens, w_value)
    score_scale = 1.0 / math.sqrt(channels)
    scores = (
        jnp.einsum("fqc,fkc->fqk", queries, keys_all, preferred_element_type=jnp.float32)
        * score_scale
    )
    largest = jnp.max(scores, axis=-1)
    weights = jnp.exp(scores - largest[..., None])
    weight_sum = jnp.sum(weights, axis=-1)
    weighted = jnp.einsum(
        "fqk,fkc->fqc",
        weights.astype(jnp.bfloat16),
        values_all,
        preferred_element_type=jnp.float32,
    )
    attended = (weighted / weight_sum[..., None]).astype(jnp.bfloat16)
    projected = jnp.einsum("ftc,cd->ftd", attended, w_output, preferred_element_type=jnp.float32)
    mixed = (
        features.astype(jnp.float32)
        + projected.reshape(frame_count, row_count, width_count, channels)
    ).astype(jnp.bfloat16)
    first_in = jax.nn.silu(rms_scale(mixed)).astype(jnp.bfloat16)
    first_pad = halo_rows(first_in, 1)
    block_out = (mixed.astype(jnp.float32) + first_cached + first_new(first_pad)).astype(
        jnp.bfloat16
    )
    block_pad = halo_rows(block_out, 1)
    upsampled = upsample_conv(block_pad, w_upsample).astype(jnp.bfloat16)
    second_in = jax.nn.silu(rms_scale(upsampled)).astype(jnp.bfloat16)
    row = lax.broadcasted_iota(jnp.int32, (1, second_in.shape[1], 1, 1), 1)
    outside = ((row == 0) & (me == 0)) | ((row == second_in.shape[1] - 1) & (me == count - 1))
    second_in = jnp.where(outside, jnp.zeros_like(second_in), second_in)
    own = upsampled[:, 1 : upsampled.shape[1] - 1]
    return (own.astype(jnp.float32) + second_cached + second_new(second_in)).astype(jnp.bfloat16)


def solution(mesh):
    placed = (
        P("grp", "ha", None, None),
        P("grp", "ha", None, None),
        P("grp", "ha", None, None),
        P(),
        P(),
        P(),
        P(),
        P(),
        P(),
        P(),
    )
    return jax.shard_map(
        per_device,
        mesh=mesh,
        in_specs=placed,
        out_specs=P("grp", "ha", None, None),
        check_vma=False,
    )
```

```python
import math

import jax
import jax.numpy as jnp
from jax import lax
from jax.sharding import PartitionSpec as P


def halo_rows(x, width):
    count, length = (lax.axis_size("ha"), x.shape[1])
    up = [(i, i + 1) for i in range(count - 1)]
    down = [(j, i) for i, j in up]
    last = lax.slice_in_dim(x, length - width, length, axis=1)
    first = lax.slice_in_dim(x, 0, width, axis=1)
    before = lax.ppermute(last, "ha", up)
    after = lax.ppermute(first, "ha", down)
    return jnp.concatenate([before, x, after], axis=1)


def cache_halos(first, second):
    count = lax.axis_size("ha")
    up = [(i, i + 1) for i in range(count - 1)]
    down = [(j, i) for i, j in up]
    frames = first.shape[0]
    last = jnp.concatenate(
        [first[:, -1:].reshape(frames, -1), second[:, -1:].reshape(frames, -1)], axis=1
    )
    head = jnp.concatenate(
        [first[:, :1].reshape(frames, -1), second[:, :1].reshape(frames, -1)], axis=1
    )
    before = lax.ppermute(last, "ha", up)
    after = lax.ppermute(head, "ha", down)
    split = first[:, :1].size // frames
    row_a, row_b = first.shape[1:], second.shape[1:]

    def rows(flat, like):
        return flat.reshape((frames, 1) + like.shape[2:])

    first_pad = jnp.concatenate(
        [rows(before[:, :split], first), first, rows(after[:, :split], first)], axis=1
    )
    second_pad = jnp.concatenate(
        [rows(before[:, split:], second), second, rows(after[:, split:], second)], axis=1
    )
    return first_pad, second_pad


def gather_rows(x):
    count = lax.axis_size("ha")
    chips = count // 2
    pieces = [x]
    for shift in range(1, chips):
        pairs = [
            (2 * c + k, 2 * ((c + shift) % chips) + k) for c in range(chips) for k in range(2)
        ]
        pieces.append(lax.ppermute(x, "ha", pairs))
    own_chip = jnp.concatenate(pieces, axis=1)
    swap = [(2 * c + k, 2 * c + 1 - k) for c in range(chips) for k in range(2)]
    other = lax.ppermute(own_chip, "ha", swap)
    return jnp.concatenate([own_chip, other], axis=1)


def rms_scale(tensor):
    widened = tensor.astype(jnp.float32)
    return widened * lax.rsqrt(jnp.mean(widened * widened, axis=-1, keepdims=True) + 1e-06)


def conv_frames(padded, weight, starts=((0, 1, 2),) * 3, rows=None):
    frames, height, width, channels = padded.shape
    out_rows = height - 2
    cols = jnp.pad(padded, ((0, 0), (0, 0), (1, 1), (0, 0)))
    result = None
    for row_off in range(3):
        if rows is None:
            window = cols[:, row_off : row_off + out_rows]
        else:
            window = jnp.stack([cols[:, r] for r in rows[row_off]], axis=1)
        stacked = jnp.concatenate(
            [window[:, :, s : s + width] for s in starts[row_off]], axis=-1
        )
        kernel = weight[row_off].reshape(3 * channels, weight.shape[-1])
        term = jnp.einsum("fhwc,cd->fhwd", stacked, kernel, preferred_element_type=jnp.float32)
        result = term if result is None else result + term
    return result


def causal_parts(cache_pad, new_pad, weight):
    zero = None
    from_cache = conv_frames(cache_pad, weight[0])
    late = conv_frames(cache_pad[1:2], weight[1])
    zero = jnp.zeros_like(late)
    from_cache = from_cache + jnp.concatenate([late, zero], axis=0)

    def from_new(pad):
        early = conv_frames(pad[0:1], weight[1])
        return conv_frames(pad, weight[2]) + jnp.concatenate([zero, early], axis=0)

    return from_cache, from_new


def project_rows(tokens, weight):
    return jnp.einsum("ftc,cd->ftd", tokens, weight, preferred_element_type=jnp.float32).astype(
        jnp.bfloat16
    )


def upsample_conv(block_pad, weight):
    rows = ((0, 0, 1, 1), (0, 1, 1, 2), (1, 1, 2, 2))
    even = conv_frames(block_pad, weight, starts=((0, 1, 1),) * 3, rows=rows)
    odd = conv_frames(block_pad, weight, starts=((1, 1, 2),) * 3, rows=rows)
    frames, height, width, channels = even.shape
    both = jnp.stack([even, odd], axis=3)
    return both.reshape(frames, height, 2 * width, channels)


def per_device(
    features,
    first_cache,
    second_cache,
    w_query,
    w_key,
    w_value,
    w_output,
    w_first,
    w_upsample,
    w_second,
):
    frame_count, row_count, width_count, channels = features.shape
    me = lax.axis_index("ha")
    count = lax.axis_size("ha")

    every_row = gather_rows(features)
    every_row, first_cache, second_cache = lax.optimization_barrier(
        (every_row, first_cache, second_cache)
    )
    first_cache_pad, second_cache_pad = cache_halos(first_cache, second_cache)
    first_cached, first_new = causal_parts(first_cache_pad, None, w_first)
    second_cached, second_new = causal_parts(second_cache_pad, None, w_second)

    normed_all = rms_scale(every_row).astype(jnp.bfloat16)
    all_tokens = normed_all.reshape(frame_count, -1, channels)
    normed = rms_scale(features).astype(jnp.bfloat16)
    normed_tokens = normed.reshape(frame_count, row_count * width_count, channels)
    queries = project_rows(normed_tokens, w_query)
    keys_all = project_rows(all_tokens, w_key)
    values_all = project_rows(all_tokens, w_value)
    score_scale = 1.0 / math.sqrt(channels)
    scores = (
        jnp.einsum("fqc,fkc->fqk", queries, keys_all, preferred_element_type=jnp.float32)
        * score_scale
    )
    largest = jnp.max(scores, axis=-1)
    weights = jnp.exp(scores - largest[..., None])
    weight_sum = jnp.sum(weights, axis=-1)
    weighted = jnp.einsum(
        "fqk,fkc->fqc",
        weights.astype(jnp.bfloat16),
        values_all,
        preferred_element_type=jnp.float32,
    )
    attended = (weighted / weight_sum[..., None]).astype(jnp.bfloat16)
    projected = jnp.einsum("ftc,cd->ftd", attended, w_output, preferred_element_type=jnp.float32)
    mixed = (
        features.astype(jnp.float32)
        + projected.reshape(frame_count, row_count, width_count, channels)
    ).astype(jnp.bfloat16)
    first_in = jax.nn.silu(rms_scale(mixed)).astype(jnp.bfloat16)
    first_pad = halo_rows(first_in, 1)
    block_out = (mixed.astype(jnp.float32) + first_cached + first_new(first_pad)).astype(
        jnp.bfloat16
    )
    block_pad = halo_rows(block_out, 1)
    upsampled = upsample_conv(block_pad, w_upsample).astype(jnp.bfloat16)
    second_in = jax.nn.silu(rms_scale(upsampled)).astype(jnp.bfloat16)
    row = lax.broadcasted_iota(jnp.int32, (1, second_in.shape[1], 1, 1), 1)
    outside = ((row == 0) & (me == 0)) | ((row == second_in.shape[1] - 1) & (me == count - 1))
    second_in = jnp.where(outside, jnp.zeros_like(second_in), second_in)
    own = upsampled[:, 1 : upsampled.shape[1] - 1]
    return (own.astype(jnp.float32) + second_cached + second_new(second_in)).astype(jnp.bfloat16)


def solution(mesh):
    placed = (
        P("grp", "ha", None, None),
        P("grp", "ha", None, None),
        P("grp", "ha", None, None),
        P(),
        P(),
        P(),
        P(),
        P(),
        P(),
        P(),
    )
    return jax.shard_map(
        per_device,
        mesh=mesh,
        in_specs=placed,
        out_specs=P("grp", "ha", None, None),
        check_vma=False,
    )
```

```python
import math

import jax
import jax.numpy as jnp
from jax import lax
from jax.sharding import PartitionSpec as P


def halo_rows(x, dim, width):
    count, length = (lax.axis_size("ha"), x.shape[dim])
    up = [(i, i + 1) for i in range(count - 1)]
    down = [(j, i) for i, j in up]
    last = lax.slice_in_dim(x, length - width, length, axis=dim)
    first = lax.slice_in_dim(x, 0, width, axis=dim)
    before = lax.ppermute(last, "ha", up)
    after = lax.ppermute(first, "ha", down)
    return before, after


def extended(x, dim, width):
    before, after = halo_rows(x, dim, width)
    return jnp.concatenate([before, x, after], axis=dim)


def joint_halo(block, cache):
    count = lax.axis_size("ha")
    up = [(i, i + 1) for i in range(count - 1)]
    down = [(j, i) for i, j in up]
    frames = block.shape[0]

    def flat(rows):
        return rows.reshape(frames, -1)

    last = jnp.concatenate([flat(block[:, -1:]), flat(cache[:, -1:])], axis=1)
    head = jnp.concatenate([flat(block[:, :1]), flat(cache[:, :1])], axis=1)
    before = lax.ppermute(last, "ha", up)
    after = lax.ppermute(head, "ha", down)
    split = block[:, :1].size // frames

    def rows(part, like):
        return part.reshape((frames, 1) + like.shape[2:])

    block_pad = jnp.concatenate(
        [rows(before[:, :split], block), block, rows(after[:, :split], block)], axis=1
    )
    cache_pad = jnp.concatenate(
        [rows(before[:, split:], cache), cache, rows(after[:, split:], cache)], axis=1
    )
    return block_pad, cache_pad


def conv_rows(padded, weight, starts, rows):
    width = padded.shape[2]
    channels = padded.shape[3]
    cols = jnp.pad(padded, ((0, 0), (0, 0), (1, 1), (0, 0)))
    result = None
    for row_off in range(3):
        window = jnp.stack([cols[:, r] for r in rows[row_off]], axis=1)
        stacked = jnp.concatenate([window[:, :, s : s + width] for s in starts], axis=-1)
        kernel = weight[row_off].reshape(3 * channels, weight.shape[-1])
        term = jnp.einsum("fhwc,cd->fhwd", stacked, kernel, preferred_element_type=jnp.float32)
        result = term if result is None else result + term
    return result


def upsample_conv(block_pad, weight):
    rows = ((0, 0, 1, 1), (0, 1, 1, 2), (1, 1, 2, 2))
    even = conv_rows(block_pad, weight, (0, 1, 1), rows)
    odd = conv_rows(block_pad, weight, (1, 1, 2), rows)
    frames, height, width, channels = even.shape
    both = jnp.stack([even, odd], axis=3)
    return both.reshape(frames, height, 2 * width, channels)


def gather_rows(x):
    count = lax.axis_size("ha")
    chips = count // 2
    pieces = [x]
    for shift in range(1, chips):
        pairs = [
            (2 * c + k, 2 * ((c + shift) % chips) + k) for c in range(chips) for k in range(2)
        ]
        pieces.append(lax.ppermute(x, "ha", pairs))
    own_chip = jnp.concatenate(pieces, axis=1)
    swap = [(2 * c + k, 2 * c + 1 - k) for c in range(chips) for k in range(2)]
    other = lax.ppermute(own_chip, "ha", swap)
    return jnp.concatenate([own_chip, other], axis=1)


def rms_scale(tensor):
    widened = tensor.astype(jnp.float32)
    return widened * lax.rsqrt(jnp.mean(widened * widened, axis=-1, keepdims=True) + 1e-06)


def conv_taps(padded, weight, time_taps):
    frames_out = padded.shape[0] - time_taps + 1
    height_out = padded.shape[1] - 2
    width_out = padded.shape[2]
    in_channels = weight.shape[-2]
    out_channels = weight.shape[-1]
    widened = jnp.pad(padded, ((0, 0), (0, 0), (1, 1), (0, 0)))
    result = jnp.zeros((frames_out, height_out, width_out, out_channels), jnp.float32)
    for time_off in range(time_taps):
        for row_off in range(3):
            window = widened[time_off : time_off + frames_out, row_off : row_off + height_out]
            stacked = jnp.concatenate(
                [window[:, :, col_off : col_off + width_out] for col_off in range(3)], axis=-1
            )
            kernel = weight[time_off, row_off].reshape(3 * in_channels, out_channels)
            result = result + jnp.einsum(
                "fhwc,cd->fhwd", stacked, kernel, preferred_element_type=jnp.float32
            )
    return result


def project_rows(tokens, weight):
    return jnp.einsum("ftc,cd->ftd", tokens, weight, preferred_element_type=jnp.float32).astype(
        jnp.bfloat16
    )


def per_device(
    features,
    first_cache,
    second_cache,
    w_query,
    w_key,
    w_value,
    w_output,
    w_first,
    w_upsample,
    w_second,
):
    frame_count, row_count, width_count, channels = features.shape
    every_row = gather_rows(features)
    normed_all = rms_scale(every_row).astype(jnp.bfloat16)
    all_tokens = normed_all.reshape(frame_count, -1, channels)
    normed = rms_scale(features).astype(jnp.bfloat16)
    normed_tokens = normed.reshape(frame_count, row_count * width_count, channels)
    queries = project_rows(normed_tokens, w_query)
    keys_all = project_rows(all_tokens, w_key)
    values_all = project_rows(all_tokens, w_value)
    score_scale = 1.0 / math.sqrt(channels)
    scores = (
        jnp.einsum("fqc,fkc->fqk", queries, keys_all, preferred_element_type=jnp.float32)
        * score_scale
    )
    largest = jnp.max(scores, axis=-1)
    weights = jnp.exp(scores - largest[..., None])
    weight_sum = jnp.sum(weights, axis=-1)
    weighted = jnp.einsum(
        "fqk,fkc->fqc",
        weights.astype(jnp.bfloat16),
        values_all,
        preferred_element_type=jnp.float32,
    )
    attended = (weighted / weight_sum[..., None]).astype(jnp.bfloat16)
    projected = jnp.einsum("ftc,cd->ftd", attended, w_output, preferred_element_type=jnp.float32)
    mixed = (
        features.astype(jnp.float32)
        + projected.reshape(frame_count, row_count, width_count, channels)
    ).astype(jnp.bfloat16)
    first_in = jax.nn.silu(rms_scale(mixed)).astype(jnp.bfloat16)
    first_stack = jnp.concatenate([first_cache, first_in], axis=0)
    first_padded = extended(first_stack, 1, 1)
    block_out = (mixed.astype(jnp.float32) + conv_taps(first_padded, w_first, 3)).astype(
        jnp.bfloat16
    )
    block_pad, cache_pad = joint_halo(block_out, second_cache)
    upsampled = upsample_conv(block_pad, w_upsample).astype(jnp.bfloat16)
    second_in = jax.nn.silu(rms_scale(upsampled)).astype(jnp.bfloat16)
    me = lax.axis_index("ha")
    count = lax.axis_size("ha")
    row = lax.broadcasted_iota(jnp.int32, (1, second_in.shape[1], 1, 1), 1)
    outside = ((row == 0) & (me == 0)) | ((row == second_in.shape[1] - 1) & (me == count - 1))
    second_in = jnp.where(outside, jnp.zeros_like(second_in), second_in)
    second_padded = jnp.concatenate([cache_pad, second_in], axis=0)
    own = upsampled[:, 1 : upsampled.shape[1] - 1]
    return (own.astype(jnp.float32) + conv_taps(second_padded, w_second, 3)).astype(
        jnp.bfloat16
    )


def solution(mesh):
    placed = (
        P("grp", "ha", None, None),
        P("grp", "ha", None, None),
        P("grp", "ha", None, None),
        P(),
        P(),
        P(),
        P(),
        P(),
        P(),
        P(),
    )
    return jax.shard_map(
        per_device,
        mesh=mesh,
        in_specs=placed,
        out_specs=P("grp", "ha", None, None),
        check_vma=False,
    )
```

```python
import math

import jax
import jax.numpy as jnp
from jax import lax
from jax.sharding import PartitionSpec as P


def halo_rows(x, dim, width):
    count, length = (lax.axis_size("ha"), x.shape[dim])
    up = [(i, i + 1) for i in range(count - 1)]
    down = [(j, i) for i, j in up]
    last = lax.slice_in_dim(x, length - width, length, axis=dim)
    first = lax.slice_in_dim(x, 0, width, axis=dim)
    before = lax.ppermute(last, "ha", up)
    after = lax.ppermute(first, "ha", down)
    return before, after


def extended(x, dim, width):
    before, after = halo_rows(x, dim, width)
    return jnp.concatenate([before, x, after], axis=dim)


def gather_rows(x):
    count = lax.axis_size("ha")
    chips = count // 2
    pieces = [x]
    for shift in range(1, chips):
        pairs = [
            (2 * c + k, 2 * ((c + shift) % chips) + k) for c in range(chips) for k in range(2)
        ]
        pieces.append(lax.ppermute(x, "ha", pairs))
    own_chip = jnp.concatenate(pieces, axis=1)
    swap = [(2 * c + k, 2 * c + 1 - k) for c in range(chips) for k in range(2)]
    other = lax.ppermute(own_chip, "ha", swap)
    return jnp.concatenate([own_chip, other], axis=1)


def rms_scale(tensor):
    widened = tensor.astype(jnp.float32)
    return widened * lax.rsqrt(jnp.mean(widened * widened, axis=-1, keepdims=True) + 1e-06)


def conv_taps(padded, weight, time_taps, rows=None):
    frames_out = padded.shape[0] - time_taps + 1
    height_out = padded.shape[1] - 2 if rows is None else len(rows[0])
    width_out = padded.shape[2]
    in_channels = weight.shape[-2]
    out_channels = weight.shape[-1]
    widened = jnp.pad(padded, ((0, 0), (0, 0), (1, 1), (0, 0)))
    result = jnp.zeros((frames_out, height_out, width_out, out_channels), jnp.float32)
    for time_off in range(time_taps):
        for row_off in range(3):
            if rows is None:
                window = widened[time_off : time_off + frames_out, row_off : row_off + height_out]
            else:
                window = jnp.stack(
                    [widened[time_off : time_off + frames_out, r] for r in rows[row_off]], axis=1
                )
            stacked = jnp.concatenate(
                [window[:, :, col_off : col_off + width_out] for col_off in range(3)], axis=-1
            )
            kernel = weight[time_off, row_off].reshape(3 * in_channels, out_channels)
            result = result + jnp.einsum(
                "fhwc,cd->fhwd", stacked, kernel, preferred_element_type=jnp.float32
            )
    return result


def project_rows(tokens, weight):
    return jnp.einsum("ftc,cd->ftd", tokens, weight, preferred_element_type=jnp.float32).astype(
        jnp.bfloat16
    )


def per_device(
    features,
    first_cache,
    second_cache,
    w_query,
    w_key,
    w_value,
    w_output,
    w_first,
    w_upsample,
    w_second,
):
    frame_count, row_count, width_count, channels = features.shape
    every_row = gather_rows(features)
    normed_all = rms_scale(every_row).astype(jnp.bfloat16)
    all_tokens = normed_all.reshape(frame_count, -1, channels)
    normed = rms_scale(features).astype(jnp.bfloat16)
    normed_tokens = normed.reshape(frame_count, row_count * width_count, channels)
    queries = project_rows(normed_tokens, w_query)
    keys_all = project_rows(all_tokens, w_key)
    values_all = project_rows(all_tokens, w_value)
    score_scale = 1.0 / math.sqrt(channels)
    scores = (
        jnp.einsum("fqc,fkc->fqk", queries, keys_all, preferred_element_type=jnp.float32)
        * score_scale
    )
    largest = jnp.max(scores, axis=-1)
    weights = jnp.exp(scores - largest[..., None])
    weight_sum = jnp.sum(weights, axis=-1)
    weighted = jnp.einsum(
        "fqk,fkc->fqc",
        weights.astype(jnp.bfloat16),
        values_all,
        preferred_element_type=jnp.float32,
    )
    attended = (weighted / weight_sum[..., None]).astype(jnp.bfloat16)
    projected = jnp.einsum("ftc,cd->ftd", attended, w_output, preferred_element_type=jnp.float32)
    mixed = (
        features.astype(jnp.float32)
        + projected.reshape(frame_count, row_count, width_count, channels)
    ).astype(jnp.bfloat16)
    first_in = jax.nn.silu(rms_scale(mixed)).astype(jnp.bfloat16)
    first_stack = jnp.concatenate([first_cache, first_in], axis=0)
    first_padded = extended(first_stack, 1, 1)
    second_cache_pad = extended(second_cache, 1, 1)
    block_out = (mixed.astype(jnp.float32) + conv_taps(first_padded, w_first, 3)).astype(
        jnp.bfloat16
    )
    block_padded = extended(block_out, 1, 1)
    widened = jnp.repeat(block_padded, 2, axis=2)
    upsampled = conv_taps(
        widened, w_upsample[None], 1, rows=((0, 0, 1, 1), (0, 1, 1, 2), (1, 1, 2, 2))
    ).astype(jnp.bfloat16)
    second_in = jax.nn.silu(rms_scale(upsampled)).astype(jnp.bfloat16)
    me = lax.axis_index("ha")
    count = lax.axis_size("ha")
    row = lax.broadcasted_iota(jnp.int32, (1, second_in.shape[1], 1, 1), 1)
    outside = ((row == 0) & (me == 0)) | ((row == second_in.shape[1] - 1) & (me == count - 1))
    second_in = jnp.where(outside, jnp.zeros_like(second_in), second_in)
    second_padded = jnp.concatenate([second_cache_pad, second_in], axis=0)
    own = upsampled[:, 1 : upsampled.shape[1] - 1]
    return (own.astype(jnp.float32) + conv_taps(second_padded, w_second, 3)).astype(
        jnp.bfloat16
    )


def solution(mesh):
    placed = (
        P("grp", "ha", None, None),
        P("grp", "ha", None, None),
        P("grp", "ha", None, None),
        P(),
        P(),
        P(),
        P(),
        P(),
        P(),
        P(),
    )
    return jax.shard_map(
        per_device,
        mesh=mesh,
        in_specs=placed,
        out_specs=P("grp", "ha", None, None),
        check_vma=False,
    )
```

```python
import math

import jax
import jax.numpy as jnp
from jax import lax
from jax.sharding import PartitionSpec as P


def halo_rows(x, dim, width):
    count, length = (lax.axis_size("ha"), x.shape[dim])
    up = [(i, i + 1) for i in range(count - 1)]
    down = [(j, i) for i, j in up]
    last = lax.slice_in_dim(x, length - width, length, axis=dim)
    first = lax.slice_in_dim(x, 0, width, axis=dim)
    before = lax.ppermute(last, "ha", up)
    after = lax.ppermute(first, "ha", down)
    return before, after


def extended(x, dim, width):
    before, after = halo_rows(x, dim, width)
    return jnp.concatenate([before, x, after], axis=dim)


def gather_rows(x):
    count = lax.axis_size("ha")
    chips = count // 2
    pieces = [x]
    for shift in range(1, chips):
        pairs = [
            (2 * c + k, 2 * ((c + shift) % chips) + k) for c in range(chips) for k in range(2)
        ]
        pieces.append(lax.ppermute(x, "ha", pairs))
    own_chip = jnp.concatenate(pieces, axis=1)
    swap = [(2 * c + k, 2 * c + 1 - k) for c in range(chips) for k in range(2)]
    other = lax.ppermute(own_chip, "ha", swap)
    return jnp.concatenate([own_chip, other], axis=1)


def rms_scale(tensor):
    widened = tensor.astype(jnp.float32)
    return widened * lax.rsqrt(jnp.mean(widened * widened, axis=-1, keepdims=True) + 1e-06)


def conv_taps(padded, weight, time_taps):
    frames_out = padded.shape[0] - time_taps + 1
    height_out = padded.shape[1] - 2
    width_out = padded.shape[2]
    in_channels = weight.shape[-2]
    out_channels = weight.shape[-1]
    widened = jnp.pad(padded, ((0, 0), (0, 0), (1, 1), (0, 0)))
    result = jnp.zeros((frames_out, height_out, width_out, out_channels), jnp.float32)
    for time_off in range(time_taps):
        for row_off in range(3):
            window = widened[time_off : time_off + frames_out, row_off : row_off + height_out]
            stacked = jnp.concatenate(
                [window[:, :, col_off : col_off + width_out] for col_off in range(3)], axis=-1
            )
            kernel = weight[time_off, row_off].reshape(3 * in_channels, out_channels)
            result = result + jnp.einsum(
                "fhwc,cd->fhwd", stacked, kernel, preferred_element_type=jnp.float32
            )
    return result


def project_rows(tokens, weight):
    return jnp.einsum("ftc,cd->ftd", tokens, weight, preferred_element_type=jnp.float32).astype(
        jnp.bfloat16
    )


def per_device(
    features,
    first_cache,
    second_cache,
    w_query,
    w_key,
    w_value,
    w_output,
    w_first,
    w_upsample,
    w_second,
):
    frame_count, row_count, width_count, channels = features.shape
    every_row = gather_rows(features)
    normed_all = rms_scale(every_row).astype(jnp.bfloat16)
    all_tokens = normed_all.reshape(frame_count, -1, channels)
    normed = rms_scale(features).astype(jnp.bfloat16)
    normed_tokens = normed.reshape(frame_count, row_count * width_count, channels)
    queries = project_rows(normed_tokens, w_query)
    keys_all = project_rows(all_tokens, w_key)
    values_all = project_rows(all_tokens, w_value)
    keys_all, values_all = lax.optimization_barrier((keys_all, values_all))
    score_scale = 1.0 / math.sqrt(channels)
    scores = (
        jnp.einsum("fqc,fkc->fqk", queries, keys_all, preferred_element_type=jnp.float32)
        * score_scale
    )
    largest = jnp.max(scores, axis=-1)
    weights = jnp.exp(scores - largest[..., None])
    weight_sum = jnp.sum(weights, axis=-1)
    weighted = jnp.einsum(
        "fqk,fkc->fqc",
        weights.astype(jnp.bfloat16),
        values_all,
        preferred_element_type=jnp.float32,
    )
    attended = (weighted / weight_sum[..., None]).astype(jnp.bfloat16)
    projected = jnp.einsum("ftc,cd->ftd", attended, w_output, preferred_element_type=jnp.float32)
    mixed = (
        features.astype(jnp.float32)
        + projected.reshape(frame_count, row_count, width_count, channels)
    ).astype(jnp.bfloat16)
    first_in = jax.nn.silu(rms_scale(mixed)).astype(jnp.bfloat16)
    first_stack = jnp.concatenate([first_cache, first_in], axis=0)
    first_padded = extended(first_stack, 1, 1)
    block_out = (mixed.astype(jnp.float32) + conv_taps(first_padded, w_first, 3)).astype(
        jnp.bfloat16
    )
    block_padded = extended(block_out, 1, 1)
    enlarged = jnp.repeat(jnp.repeat(block_padded, 2, axis=1), 2, axis=2)
    up_padded = enlarged[:, 1 : enlarged.shape[1] - 1]
    upsampled = conv_taps(up_padded, w_upsample[None], 1).astype(jnp.bfloat16)
    second_in = jax.nn.silu(rms_scale(upsampled)).astype(jnp.bfloat16)
    second_stack = jnp.concatenate([second_cache, second_in], axis=0)
    second_padded = extended(second_stack, 1, 1)
    return (upsampled.astype(jnp.float32) + conv_taps(second_padded, w_second, 3)).astype(
        jnp.bfloat16
    )


def solution(mesh):
    placed = (
        P("grp", "ha", None, None),
        P("grp", "ha", None, None),
        P("grp", "ha", None, None),
        P(),
        P(),
        P(),
        P(),
        P(),
        P(),
        P(),
    )
    return jax.shard_map(
        per_device,
        mesh=mesh,
        in_specs=placed,
        out_specs=P("grp", "ha", None, None),
        check_vma=False,
    )
```

```python
import math

import jax
import jax.numpy as jnp
from jax import lax
from jax.sharding import PartitionSpec as P


def halo_rows(x, dim, width):
    count, length = (lax.axis_size("ha"), x.shape[dim])
    up = [(i, i + 1) for i in range(count - 1)]
    down = [(j, i) for i, j in up]
    last = lax.slice_in_dim(x, length - width, length, axis=dim)
    first = lax.slice_in_dim(x, 0, width, axis=dim)
    before = lax.ppermute(last, "ha", up)
    after = lax.ppermute(first, "ha", down)
    return before, after


def extended(x, dim, width):
    before, after = halo_rows(x, dim, width)
    return jnp.concatenate([before, x, after], axis=dim)


def gather_rows(x):
    count = lax.axis_size("ha")
    chips = count // 2
    pieces = [x]
    for shift in range(1, chips):
        pairs = [
            (2 * c + k, 2 * ((c + shift) % chips) + k) for c in range(chips) for k in range(2)
        ]
        pieces.append(lax.ppermute(x, "ha", pairs))
    own_chip = jnp.concatenate(pieces, axis=1)
    swap = [(2 * c + k, 2 * c + 1 - k) for c in range(chips) for k in range(2)]
    other = lax.ppermute(own_chip, "ha", swap)
    return jnp.concatenate([own_chip, other], axis=1)


def rms_scale(tensor):
    widened = tensor.astype(jnp.float32)
    return widened * lax.rsqrt(jnp.mean(widened * widened, axis=-1, keepdims=True) + 1e-06)


def conv_taps(padded, weight, time_taps, rows=None):
    frames_out = padded.shape[0] - time_taps + 1
    height_out = padded.shape[1] - 2 if rows is None else len(rows[0])
    width_out = padded.shape[2]
    in_channels = weight.shape[-2]
    out_channels = weight.shape[-1]
    widened = jnp.pad(padded, ((0, 0), (0, 0), (1, 1), (0, 0)))
    result = jnp.zeros((frames_out, height_out, width_out, out_channels), jnp.float32)
    for time_off in range(time_taps):
        for row_off in range(3):
            if rows is None:
                window = widened[time_off : time_off + frames_out, row_off : row_off + height_out]
            else:
                window = jnp.stack(
                    [widened[time_off : time_off + frames_out, r] for r in rows[row_off]], axis=1
                )
            stacked = jnp.concatenate(
                [window[:, :, col_off : col_off + width_out] for col_off in range(3)], axis=-1
            )
            kernel = weight[time_off, row_off].reshape(3 * in_channels, out_channels)
            result = result + jnp.einsum(
                "fhwc,cd->fhwd", stacked, kernel, preferred_element_type=jnp.float32
            )
    return result


def project_rows(tokens, weight):
    return jnp.einsum("ftc,cd->ftd", tokens, weight, preferred_element_type=jnp.float32).astype(
        jnp.bfloat16
    )


def per_device(
    features,
    first_cache,
    second_cache,
    w_query,
    w_key,
    w_value,
    w_output,
    w_first,
    w_upsample,
    w_second,
):
    frame_count, row_count, width_count, channels = features.shape
    every_row = gather_rows(features)
    every_row, first_cache, second_cache = lax.optimization_barrier(
        (every_row, first_cache, second_cache)
    )
    first_cache_pad = extended(first_cache, 1, 1)
    second_cache_pad = extended(second_cache, 1, 1)
    normed_all = rms_scale(every_row).astype(jnp.bfloat16)
    all_tokens = normed_all.reshape(frame_count, -1, channels)
    normed = rms_scale(features).astype(jnp.bfloat16)
    normed_tokens = normed.reshape(frame_count, row_count * width_count, channels)
    queries = project_rows(normed_tokens, w_query)
    keys_all = project_rows(all_tokens, w_key)
    values_all = project_rows(all_tokens, w_value)
    keys_all, values_all, first_cache_pad, second_cache_pad = lax.optimization_barrier(
        (keys_all, values_all, first_cache_pad, second_cache_pad)
    )
    score_scale = 1.0 / math.sqrt(channels)
    scores = (
        jnp.einsum("fqc,fkc->fqk", queries, keys_all, preferred_element_type=jnp.float32)
        * score_scale
    )
    largest = jnp.max(scores, axis=-1)
    weights = jnp.exp(scores - largest[..., None])
    weight_sum = jnp.sum(weights, axis=-1)
    weighted = jnp.einsum(
        "fqk,fkc->fqc",
        weights.astype(jnp.bfloat16),
        values_all,
        preferred_element_type=jnp.float32,
    )
    attended = (weighted / weight_sum[..., None]).astype(jnp.bfloat16)
    projected = jnp.einsum("ftc,cd->ftd", attended, w_output, preferred_element_type=jnp.float32)
    mixed = (
        features.astype(jnp.float32)
        + projected.reshape(frame_count, row_count, width_count, channels)
    ).astype(jnp.bfloat16)
    first_in = jax.nn.silu(rms_scale(mixed)).astype(jnp.bfloat16)
    first_padded = jnp.concatenate([first_cache_pad, extended(first_in, 1, 1)], axis=0)
    block_out = (mixed.astype(jnp.float32) + conv_taps(first_padded, w_first, 3)).astype(
        jnp.bfloat16
    )
    block_padded = extended(block_out, 1, 1)
    widened = jnp.repeat(block_padded, 2, axis=2)
    upsampled = conv_taps(widened, w_upsample[None], 1, rows=((0, 1), (1, 1), (1, 2))).astype(
        jnp.bfloat16
    )
    second_in = jax.nn.silu(rms_scale(upsampled)).astype(jnp.bfloat16)
    second_padded = jnp.concatenate([second_cache_pad, extended(second_in, 1, 1)], axis=0)
    return (upsampled.astype(jnp.float32) + conv_taps(second_padded, w_second, 3)).astype(
        jnp.bfloat16
    )


def solution(mesh):
    placed = (
        P("grp", "ha", None, None),
        P("grp", "ha", None, None),
        P("grp", "ha", None, None),
        P(),
        P(),
        P(),
        P(),
        P(),
        P(),
        P(),
    )
    return jax.shard_map(
        per_device,
        mesh=mesh,
        in_specs=placed,
        out_specs=P("grp", "ha", None, None),
        check_vma=False,
    )
```

```python
import math

import jax
import jax.numpy as jnp
from jax import lax
from jax.sharding import PartitionSpec as P


def halo_rows(x, dim, width):
    count, length = (lax.axis_size("ha"), x.shape[dim])
    up = [(i, i + 1) for i in range(count - 1)]
    down = [(j, i) for i, j in up]
    last = lax.slice_in_dim(x, length - width, length, axis=dim)
    first = lax.slice_in_dim(x, 0, width, axis=dim)
    before = lax.ppermute(last, "ha", up)
    after = lax.ppermute(first, "ha", down)
    return before, after


def extended(x, dim, width):
    before, after = halo_rows(x, dim, width)
    return jnp.concatenate([before, x, after], axis=dim)


def gather_rows(x):
    count = lax.axis_size("ha")
    chips = count // 2
    pieces = [x]
    for shift in range(1, chips):
        pairs = [
            (2 * c + k, 2 * ((c + shift) % chips) + k) for c in range(chips) for k in range(2)
        ]
        pieces.append(lax.ppermute(x, "ha", pairs))
    own_chip = jnp.concatenate(pieces, axis=1)
    swap = [(2 * c + k, 2 * c + 1 - k) for c in range(chips) for k in range(2)]
    other = lax.ppermute(own_chip, "ha", swap)
    return jnp.concatenate([own_chip, other], axis=1)


def rms_scale(tensor):
    widened = tensor.astype(jnp.float32)
    return widened * lax.rsqrt(jnp.mean(widened * widened, axis=-1, keepdims=True) + 1e-06)


def conv_taps(padded, weight, time_taps, rows=None):
    frames_out = padded.shape[0] - time_taps + 1
    height_out = padded.shape[1] - 2 if rows is None else len(rows[0])
    width_out = padded.shape[2]
    in_channels = weight.shape[-2]
    out_channels = weight.shape[-1]
    widened = jnp.pad(padded, ((0, 0), (0, 0), (1, 1), (0, 0)))
    result = jnp.zeros((frames_out, height_out, width_out, out_channels), jnp.float32)
    for time_off in range(time_taps):
        for row_off in range(3):
            if rows is None:
                window = widened[time_off : time_off + frames_out, row_off : row_off + height_out]
            else:
                window = jnp.stack(
                    [widened[time_off : time_off + frames_out, r] for r in rows[row_off]], axis=1
                )
            stacked = jnp.concatenate(
                [window[:, :, col_off : col_off + width_out] for col_off in range(3)], axis=-1
            )
            kernel = weight[time_off, row_off].reshape(3 * in_channels, out_channels)
            result = result + jnp.einsum(
                "fhwc,cd->fhwd", stacked, kernel, preferred_element_type=jnp.float32
            )
    return result


def project_rows(tokens, weight):
    return jnp.einsum("ftc,cd->ftd", tokens, weight, preferred_element_type=jnp.float32).astype(
        jnp.bfloat16
    )


def per_device(
    features,
    first_cache,
    second_cache,
    w_query,
    w_key,
    w_value,
    w_output,
    w_first,
    w_upsample,
    w_second,
):
    frame_count, row_count, width_count, channels = features.shape
    every_row = gather_rows(features)
    normed_all = rms_scale(every_row).astype(jnp.bfloat16)
    all_tokens = normed_all.reshape(frame_count, -1, channels)
    normed = rms_scale(features).astype(jnp.bfloat16)
    normed_tokens = normed.reshape(frame_count, row_count * width_count, channels)
    queries = project_rows(normed_tokens, w_query)
    keys_all = project_rows(all_tokens, w_key)
    values_all = project_rows(all_tokens, w_value)
    score_scale = 1.0 / math.sqrt(channels)
    scores = (
        jnp.einsum("fqc,fkc->fqk", queries, keys_all, preferred_element_type=jnp.float32)
        * score_scale
    )
    largest = jnp.max(scores, axis=-1)
    weights = jnp.exp(scores - largest[..., None])
    weight_sum = jnp.sum(weights, axis=-1)
    weighted = jnp.einsum(
        "fqk,fkc->fqc",
        weights.astype(jnp.bfloat16),
        values_all,
        preferred_element_type=jnp.float32,
    )
    attended = (weighted / weight_sum[..., None]).astype(jnp.bfloat16)
    projected = jnp.einsum("ftc,cd->ftd", attended, w_output, preferred_element_type=jnp.float32)
    mixed = (
        features.astype(jnp.float32)
        + projected.reshape(frame_count, row_count, width_count, channels)
    ).astype(jnp.bfloat16)
    first_in = jax.nn.silu(rms_scale(mixed)).astype(jnp.bfloat16)
    first_stack = jnp.concatenate([first_cache, first_in], axis=0)
    first_padded = extended(first_stack, 1, 1)
    block_out = (mixed.astype(jnp.float32) + conv_taps(first_padded, w_first, 3)).astype(
        jnp.bfloat16
    )
    block_padded = extended(block_out, 1, 1)
    widened = jnp.repeat(block_padded, 2, axis=2)
    upsampled = conv_taps(widened, w_upsample[None], 1, rows=((0, 1), (1, 1), (1, 2))).astype(
        jnp.bfloat16
    )
    second_in = jax.nn.silu(rms_scale(upsampled)).astype(jnp.bfloat16)
    second_stack = jnp.concatenate([second_cache, second_in], axis=0)
    second_padded = extended(second_stack, 1, 1)
    return (upsampled.astype(jnp.float32) + conv_taps(second_padded, w_second, 3)).astype(
        jnp.bfloat16
    )


def solution(mesh):
    placed = (
        P("grp", "ha", None, None),
        P("grp", "ha", None, None),
        P("grp", "ha", None, None),
        P(),
        P(),
        P(),
        P(),
        P(),
        P(),
        P(),
    )
    return jax.shard_map(
        per_device,
        mesh=mesh,
        in_specs=placed,
        out_specs=P("grp", "ha", None, None),
        check_vma=False,
    )
```

```python
import math

import jax
import jax.numpy as jnp
from jax import lax
from jax.sharding import PartitionSpec as P


def halo_rows(x, dim, width):
    count, length = (lax.axis_size("ha"), x.shape[dim])
    up = [(i, i + 1) for i in range(count - 1)]
    down = [(j, i) for i, j in up]
    last = lax.slice_in_dim(x, length - width, length, axis=dim)
    first = lax.slice_in_dim(x, 0, width, axis=dim)
    before = lax.ppermute(last, "ha", up)
    after = lax.ppermute(first, "ha", down)
    return before, after


def extended(x, dim, width):
    before, after = halo_rows(x, dim, width)
    return jnp.concatenate([before, x, after], axis=dim)


def gather_rows(x):
    count = lax.axis_size("ha")
    chips = count // 2
    pieces = [x]
    for shift in range(1, chips):
        pairs = [
            (2 * c + k, 2 * ((c + shift) % chips) + k) for c in range(chips) for k in range(2)
        ]
        pieces.append(lax.ppermute(x, "ha", pairs))
    own_chip = jnp.concatenate(pieces, axis=1)
    swap = [(2 * c + k, 2 * c + 1 - k) for c in range(chips) for k in range(2)]
    other = lax.ppermute(own_chip, "ha", swap)
    return pieces + [other]


def rms_scale(tensor):
    widened = tensor.astype(jnp.float32)
    return widened * lax.rsqrt(jnp.mean(widened * widened, axis=-1, keepdims=True) + 1e-06)


def conv_taps(padded, weight, time_taps, rows=None):
    frames_out = padded.shape[0] - time_taps + 1
    height_out = padded.shape[1] - 2 if rows is None else len(rows[0])
    width_out = padded.shape[2]
    in_channels = weight.shape[-2]
    out_channels = weight.shape[-1]
    widened = jnp.pad(padded, ((0, 0), (0, 0), (1, 1), (0, 0)))
    result = jnp.zeros((frames_out, height_out, width_out, out_channels), jnp.float32)
    for time_off in range(time_taps):
        for row_off in range(3):
            if rows is None:
                window = widened[time_off : time_off + frames_out, row_off : row_off + height_out]
            else:
                window = jnp.stack(
                    [widened[time_off : time_off + frames_out, r] for r in rows[row_off]], axis=1
                )
            stacked = jnp.concatenate(
                [window[:, :, col_off : col_off + width_out] for col_off in range(3)], axis=-1
            )
            kernel = weight[time_off, row_off].reshape(3 * in_channels, out_channels)
            result = result + jnp.einsum(
                "fhwc,cd->fhwd", stacked, kernel, preferred_element_type=jnp.float32
            )
    return result


def project_rows(tokens, weight):
    return jnp.einsum("ftc,cd->ftd", tokens, weight, preferred_element_type=jnp.float32).astype(
        jnp.bfloat16
    )


def per_device(
    features,
    first_cache,
    second_cache,
    w_query,
    w_key,
    w_value,
    w_output,
    w_first,
    w_upsample,
    w_second,
):
    frame_count, row_count, width_count, channels = features.shape
    normed = rms_scale(features).astype(jnp.bfloat16)
    normed_tokens = normed.reshape(frame_count, row_count * width_count, channels)
    queries = project_rows(normed_tokens, w_query)
    score_scale = 1.0 / math.sqrt(channels)
    score_parts, value_parts = [], []
    for piece in gather_rows(features):
        piece_tokens = rms_scale(piece).astype(jnp.bfloat16).reshape(frame_count, -1, channels)
        piece_keys = project_rows(piece_tokens, w_key)
        value_parts.append(project_rows(piece_tokens, w_value))
        score_parts.append(
            jnp.einsum("fqc,fkc->fqk", queries, piece_keys, preferred_element_type=jnp.float32)
            * score_scale
        )
    scores = jnp.concatenate(score_parts, axis=-1)
    values_all = jnp.concatenate(value_parts, axis=1)
    largest = jnp.max(scores, axis=-1)
    weights = jnp.exp(scores - largest[..., None])
    weight_sum = jnp.sum(weights, axis=-1)
    weighted = jnp.einsum(
        "fqk,fkc->fqc",
        weights.astype(jnp.bfloat16),
        values_all,
        preferred_element_type=jnp.float32,
    )
    attended = (weighted / weight_sum[..., None]).astype(jnp.bfloat16)
    projected = jnp.einsum("ftc,cd->ftd", attended, w_output, preferred_element_type=jnp.float32)
    mixed = (
        features.astype(jnp.float32)
        + projected.reshape(frame_count, row_count, width_count, channels)
    ).astype(jnp.bfloat16)
    first_in = jax.nn.silu(rms_scale(mixed)).astype(jnp.bfloat16)
    first_stack = jnp.concatenate([first_cache, first_in], axis=0)
    first_padded = extended(first_stack, 1, 1)
    block_out = (mixed.astype(jnp.float32) + conv_taps(first_padded, w_first, 3)).astype(
        jnp.bfloat16
    )
    block_padded = extended(block_out, 1, 1)
    widened = jnp.repeat(block_padded, 2, axis=2)
    upsampled = conv_taps(widened, w_upsample[None], 1, rows=((0, 1), (1, 1), (1, 2))).astype(
        jnp.bfloat16
    )
    second_in = jax.nn.silu(rms_scale(upsampled)).astype(jnp.bfloat16)
    second_stack = jnp.concatenate([second_cache, second_in], axis=0)
    second_padded = extended(second_stack, 1, 1)
    return (upsampled.astype(jnp.float32) + conv_taps(second_padded, w_second, 3)).astype(
        jnp.bfloat16
    )


def solution(mesh):
    placed = (
        P("grp", "ha", None, None),
        P("grp", "ha", None, None),
        P("grp", "ha", None, None),
        P(),
        P(),
        P(),
        P(),
        P(),
        P(),
        P(),
    )
    return jax.shard_map(
        per_device,
        mesh=mesh,
        in_specs=placed,
        out_specs=P("grp", "ha", None, None),
        check_vma=False,
    )
```

```python
import functools
import math

import jax
import jax.numpy as jnp
from jax import lax
from jax.experimental import pallas as pl
from jax.experimental.pallas import tpu as pltpu
from jax.sharding import PartitionSpec as P


def halo_rows(x, dim, width):
    count, length = (lax.axis_size("ha"), x.shape[dim])
    up = [(i, i + 1) for i in range(count - 1)]
    down = [(j, i) for i, j in up]
    last = lax.slice_in_dim(x, length - width, length, axis=dim)
    first = lax.slice_in_dim(x, 0, width, axis=dim)
    before = lax.ppermute(last, "ha", up)
    after = lax.ppermute(first, "ha", down)
    return before, after


def extended(x, dim, width):
    before, after = halo_rows(x, dim, width)
    return jnp.concatenate([before, x, after], axis=dim)


def gather_rows(x):
    count = lax.axis_size("ha")
    chips = count // 2
    pieces = [x]
    for shift in range(1, chips):
        pairs = [
            (2 * c + k, 2 * ((c + shift) % chips) + k) for c in range(chips) for k in range(2)
        ]
        pieces.append(lax.ppermute(x, "ha", pairs))
    own_chip = jnp.concatenate(pieces, axis=1)
    swap = [(2 * c + k, 2 * c + 1 - k) for c in range(chips) for k in range(2)]
    other = lax.ppermute(own_chip, "ha", swap)
    return jnp.concatenate([own_chip, other], axis=1)


def rms_scale(tensor):
    widened = tensor.astype(jnp.float32)
    return widened * lax.rsqrt(jnp.mean(widened * widened, axis=-1, keepdims=True) + 1e-06)


def conv_taps(padded, weight, time_taps, rows=None):
    frames_out = padded.shape[0] - time_taps + 1
    height_out = padded.shape[1] - 2 if rows is None else len(rows[0])
    width_out = padded.shape[2]
    in_channels = weight.shape[-2]
    out_channels = weight.shape[-1]
    widened = jnp.pad(padded, ((0, 0), (0, 0), (1, 1), (0, 0)))
    result = jnp.zeros((frames_out, height_out, width_out, out_channels), jnp.float32)
    for time_off in range(time_taps):
        for row_off in range(3):
            if rows is None:
                window = widened[time_off : time_off + frames_out, row_off : row_off + height_out]
            else:
                window = jnp.stack(
                    [widened[time_off : time_off + frames_out, r] for r in rows[row_off]], axis=1
                )
            stacked = jnp.concatenate(
                [window[:, :, col_off : col_off + width_out] for col_off in range(3)], axis=-1
            )
            kernel = weight[time_off, row_off].reshape(3 * in_channels, out_channels)
            result = result + jnp.einsum(
                "fhwc,cd->fhwd", stacked, kernel, preferred_element_type=jnp.float32
            )
    return result


def attention_kernel(scale, q_ref, k_ref, v_ref, o_ref):
    scores = (
        lax.dot_general(
            q_ref[0], k_ref[0], (((1,), (1,)), ((), ())), preferred_element_type=jnp.float32
        )
        * scale
    )
    largest = jnp.max(scores, axis=-1, keepdims=True)
    weights = jnp.exp(scores - largest)
    weight_sum = jnp.sum(weights, axis=-1, keepdims=True)
    summed = jnp.dot(weights.astype(v_ref.dtype), v_ref[0], preferred_element_type=jnp.float32)
    o_ref[0] = (summed / weight_sum).astype(o_ref.dtype)


def attend(queries, keys_all, values_all, scale):
    frames, count, channels = queries.shape
    tokens = keys_all.shape[1]
    flops = 4 * frames * count * tokens * channels
    moved = 2 * (queries.size * 2 + keys_all.size + values_all.size)
    return pl.pallas_call(
        functools.partial(attention_kernel, scale),
        grid=(frames,),
        in_specs=[
            pl.BlockSpec((1, count, channels), lambda f: (f, 0, 0)),
            pl.BlockSpec((1, tokens, channels), lambda f: (f, 0, 0)),
            pl.BlockSpec((1, tokens, channels), lambda f: (f, 0, 0)),
        ],
        out_specs=pl.BlockSpec((1, count, channels), lambda f: (f, 0, 0)),
        out_shape=jax.ShapeDtypeStruct(queries.shape, queries.dtype),
        compiler_params=pltpu.CompilerParams(vmem_limit_bytes=60 * 1024 * 1024),
        cost_estimate=pl.CostEstimate(
            flops=flops, transcendentals=frames * count * tokens, bytes_accessed=moved
        ),
    )(queries, keys_all, values_all)


def project_rows(tokens, weight):
    return jnp.einsum("ftc,cd->ftd", tokens, weight, preferred_element_type=jnp.float32).astype(
        jnp.bfloat16
    )


def per_device(
    features,
    first_cache,
    second_cache,
    w_query,
    w_key,
    w_value,
    w_output,
    w_first,
    w_upsample,
    w_second,
):
    frame_count, row_count, width_count, channels = features.shape
    every_row = gather_rows(features)
    normed_all = rms_scale(every_row).astype(jnp.bfloat16)
    all_tokens = normed_all.reshape(frame_count, -1, channels)
    normed = rms_scale(features).astype(jnp.bfloat16)
    normed_tokens = normed.reshape(frame_count, row_count * width_count, channels)
    queries = project_rows(normed_tokens, w_query)
    keys_all = project_rows(all_tokens, w_key)
    values_all = project_rows(all_tokens, w_value)
    score_scale = 1.0 / math.sqrt(channels)
    attended = attend(queries, keys_all, values_all, score_scale)
    projected = jnp.einsum("ftc,cd->ftd", attended, w_output, preferred_element_type=jnp.float32)
    mixed = (
        features.astype(jnp.float32)
        + projected.reshape(frame_count, row_count, width_count, channels)
    ).astype(jnp.bfloat16)
    first_in = jax.nn.silu(rms_scale(mixed)).astype(jnp.bfloat16)
    first_stack = jnp.concatenate([first_cache, first_in], axis=0)
    first_padded = extended(first_stack, 1, 1)
    block_out = (mixed.astype(jnp.float32) + conv_taps(first_padded, w_first, 3)).astype(
        jnp.bfloat16
    )
    block_padded = extended(block_out, 1, 1)
    widened = jnp.repeat(block_padded, 2, axis=2)
    upsampled = conv_taps(widened, w_upsample[None], 1, rows=((0, 1), (1, 1), (1, 2))).astype(
        jnp.bfloat16
    )
    second_in = jax.nn.silu(rms_scale(upsampled)).astype(jnp.bfloat16)
    second_stack = jnp.concatenate([second_cache, second_in], axis=0)
    second_padded = extended(second_stack, 1, 1)
    return (upsampled.astype(jnp.float32) + conv_taps(second_padded, w_second, 3)).astype(
        jnp.bfloat16
    )


def solution(mesh):
    placed = (
        P("grp", "ha", None, None),
        P("grp", "ha", None, None),
        P("grp", "ha", None, None),
        P(),
        P(),
        P(),
        P(),
        P(),
        P(),
        P(),
    )
    return jax.shard_map(
        per_device,
        mesh=mesh,
        in_specs=placed,
        out_specs=P("grp", "ha", None, None),
        check_vma=False,
    )
```

```python
import functools
import math

import jax
import jax.numpy as jnp
from jax import lax
from jax.experimental import pallas as pl
from jax.experimental.pallas import tpu as pltpu
from jax.sharding import PartitionSpec as P


def halo_rows(x, dim, width):
    count, length = (lax.axis_size("ha"), x.shape[dim])
    up = [(i, i + 1) for i in range(count - 1)]
    down = [(j, i) for i, j in up]
    last = lax.slice_in_dim(x, length - width, length, axis=dim)
    first = lax.slice_in_dim(x, 0, width, axis=dim)
    before = lax.ppermute(last, "ha", up)
    after = lax.ppermute(first, "ha", down)
    return before, after


def extended(x, dim, width):
    before, after = halo_rows(x, dim, width)
    return jnp.concatenate([before, x, after], axis=dim)


def gather_rows(x):
    count = lax.axis_size("ha")
    chips = count // 2
    pieces = [x]
    for shift in range(1, chips):
        pairs = [
            (2 * c + k, 2 * ((c + shift) % chips) + k) for c in range(chips) for k in range(2)
        ]
        pieces.append(lax.ppermute(x, "ha", pairs))
    own_chip = jnp.concatenate(pieces, axis=1)
    swap = [(2 * c + k, 2 * c + 1 - k) for c in range(chips) for k in range(2)]
    other = lax.ppermute(own_chip, "ha", swap)
    return jnp.concatenate([own_chip, other], axis=1)


def rms_scale(tensor):
    widened = tensor.astype(jnp.float32)
    return widened * lax.rsqrt(jnp.mean(widened * widened, axis=-1, keepdims=True) + 1e-06)


def conv_taps(padded, weight, time_taps, rows=None):
    frames_out = padded.shape[0] - time_taps + 1
    height_out = padded.shape[1] - 2 if rows is None else len(rows[0])
    width_out = padded.shape[2]
    in_channels = weight.shape[-2]
    out_channels = weight.shape[-1]
    widened = jnp.pad(padded, ((0, 0), (0, 0), (1, 1), (0, 0)))
    result = jnp.zeros((frames_out, height_out, width_out, out_channels), jnp.float32)
    for time_off in range(time_taps):
        for row_off in range(3):
            if rows is None:
                window = widened[time_off : time_off + frames_out, row_off : row_off + height_out]
            else:
                window = jnp.stack(
                    [widened[time_off : time_off + frames_out, r] for r in rows[row_off]], axis=1
                )
            stacked = jnp.concatenate(
                [window[:, :, col_off : col_off + width_out] for col_off in range(3)], axis=-1
            )
            kernel = weight[time_off, row_off].reshape(3 * in_channels, out_channels)
            result = result + jnp.einsum(
                "fhwc,cd->fhwd", stacked, kernel, preferred_element_type=jnp.float32
            )
    return result


def attention_kernel(scale, q_ref, k_ref, v_ref, o_ref):
    scores = (
        jnp.dot(q_ref[0], k_ref[0], preferred_element_type=jnp.float32) * scale
    )
    largest = jnp.max(scores, axis=-1, keepdims=True)
    weights = jnp.exp(scores - largest)
    weight_sum = jnp.sum(weights, axis=-1, keepdims=True)
    summed = jnp.dot(weights.astype(v_ref.dtype), v_ref[0], preferred_element_type=jnp.float32)
    o_ref[0] = (summed / weight_sum).astype(o_ref.dtype)


def attend(queries, keys_all, values_all, scale):
    frames, count, channels = queries.shape
    tokens = keys_all.shape[2]
    flops = 4 * frames * count * tokens * channels
    moved = 2 * (queries.size * 2 + keys_all.size + values_all.size)
    return pl.pallas_call(
        functools.partial(attention_kernel, scale),
        grid=(frames,),
        in_specs=[
            pl.BlockSpec((1, count, channels), lambda f: (f, 0, 0)),
            pl.BlockSpec((1, channels, tokens), lambda f: (f, 0, 0)),
            pl.BlockSpec((1, tokens, channels), lambda f: (f, 0, 0)),
        ],
        out_specs=pl.BlockSpec((1, count, channels), lambda f: (f, 0, 0)),
        out_shape=jax.ShapeDtypeStruct(queries.shape, queries.dtype),
        compiler_params=pltpu.CompilerParams(vmem_limit_bytes=60 * 1024 * 1024),
        cost_estimate=pl.CostEstimate(
            flops=flops, transcendentals=frames * count * tokens, bytes_accessed=moved
        ),
    )(queries, keys_all, values_all)


def project_rows(tokens, weight):
    return jnp.einsum("ftc,cd->ftd", tokens, weight, preferred_element_type=jnp.float32).astype(
        jnp.bfloat16
    )


def per_device(
    features,
    first_cache,
    second_cache,
    w_query,
    w_key,
    w_value,
    w_output,
    w_first,
    w_upsample,
    w_second,
):
    frame_count, row_count, width_count, channels = features.shape
    every_row = gather_rows(features)
    normed_all = rms_scale(every_row).astype(jnp.bfloat16)
    all_tokens = normed_all.reshape(frame_count, -1, channels)
    normed = rms_scale(features).astype(jnp.bfloat16)
    normed_tokens = normed.reshape(frame_count, row_count * width_count, channels)
    queries = project_rows(normed_tokens, w_query)
    keys_all = jnp.einsum(
        "ftc,cd->fdt", all_tokens, w_key, preferred_element_type=jnp.float32
    ).astype(jnp.bfloat16)
    values_all = project_rows(all_tokens, w_value)
    score_scale = 1.0 / math.sqrt(channels)
    attended = attend(queries, keys_all, values_all, score_scale)
    projected = jnp.einsum("ftc,cd->ftd", attended, w_output, preferred_element_type=jnp.float32)
    mixed = (
        features.astype(jnp.float32)
        + projected.reshape(frame_count, row_count, width_count, channels)
    ).astype(jnp.bfloat16)
    first_in = jax.nn.silu(rms_scale(mixed)).astype(jnp.bfloat16)
    first_stack = jnp.concatenate([first_cache, first_in], axis=0)
    first_padded = extended(first_stack, 1, 1)
    block_out = (mixed.astype(jnp.float32) + conv_taps(first_padded, w_first, 3)).astype(
        jnp.bfloat16
    )
    block_padded = extended(block_out, 1, 1)
    widened = jnp.repeat(block_padded, 2, axis=2)
    upsampled = conv_taps(widened, w_upsample[None], 1, rows=((0, 1), (1, 1), (1, 2))).astype(
        jnp.bfloat16
    )
    second_in = jax.nn.silu(rms_scale(upsampled)).astype(jnp.bfloat16)
    second_stack = jnp.concatenate([second_cache, second_in], axis=0)
    second_padded = extended(second_stack, 1, 1)
    return (upsampled.astype(jnp.float32) + conv_taps(second_padded, w_second, 3)).astype(
        jnp.bfloat16
    )


def solution(mesh):
    placed = (
        P("grp", "ha", None, None),
        P("grp", "ha", None, None),
        P("grp", "ha", None, None),
        P(),
        P(),
        P(),
        P(),
        P(),
        P(),
        P(),
    )
    return jax.shard_map(
        per_device,
        mesh=mesh,
        in_specs=placed,
        out_specs=P("grp", "ha", None, None),
        check_vma=False,
    )
```

```python
import functools
import math

import jax
import jax.numpy as jnp
from jax import lax
from jax.experimental import pallas as pl
from jax.experimental.pallas import tpu as pltpu
from jax.sharding import PartitionSpec as P


def halo_rows(x, dim, width):
    count, length = (lax.axis_size("ha"), x.shape[dim])
    up = [(i, i + 1) for i in range(count - 1)]
    down = [(j, i) for i, j in up]
    last = lax.slice_in_dim(x, length - width, length, axis=dim)
    first = lax.slice_in_dim(x, 0, width, axis=dim)
    before = lax.ppermute(last, "ha", up)
    after = lax.ppermute(first, "ha", down)
    return before, after


def extended(x, dim, width):
    before, after = halo_rows(x, dim, width)
    return jnp.concatenate([before, x, after], axis=dim)


def gather_chip_rows(x):
    count = lax.axis_size("ha")
    chips = count // 2
    pieces = [x]
    for shift in range(1, chips):
        pairs = [
            (2 * c + k, 2 * ((c + shift) % chips) + k) for c in range(chips) for k in range(2)
        ]
        pieces.append(lax.ppermute(x, "ha", pairs))
    return jnp.concatenate(pieces, axis=1)


def gather_rows(x):
    count = lax.axis_size("ha")
    chips = count // 2
    pieces = [x]
    for shift in range(1, chips):
        pairs = [
            (2 * c + k, 2 * ((c + shift) % chips) + k) for c in range(chips) for k in range(2)
        ]
        pieces.append(lax.ppermute(x, "ha", pairs))
    own_chip = jnp.concatenate(pieces, axis=1)
    swap = [(2 * c + k, 2 * c + 1 - k) for c in range(chips) for k in range(2)]
    other = lax.ppermute(own_chip, "ha", swap)
    return jnp.concatenate([own_chip, other], axis=1)


def rms_scale(tensor):
    widened = tensor.astype(jnp.float32)
    return widened * lax.rsqrt(jnp.mean(widened * widened, axis=-1, keepdims=True) + 1e-06)


def conv_taps(padded, weight, time_taps, rows=None):
    frames_out = padded.shape[0] - time_taps + 1
    height_out = padded.shape[1] - 2 if rows is None else len(rows[0])
    width_out = padded.shape[2]
    in_channels = weight.shape[-2]
    out_channels = weight.shape[-1]
    widened = jnp.pad(padded, ((0, 0), (0, 0), (1, 1), (0, 0)))
    result = jnp.zeros((frames_out, height_out, width_out, out_channels), jnp.float32)
    for time_off in range(time_taps):
        for row_off in range(3):
            if rows is None:
                window = widened[time_off : time_off + frames_out, row_off : row_off + height_out]
            else:
                window = jnp.stack(
                    [widened[time_off : time_off + frames_out, r] for r in rows[row_off]], axis=1
                )
            stacked = jnp.concatenate(
                [window[:, :, col_off : col_off + width_out] for col_off in range(3)], axis=-1
            )
            kernel = weight[time_off, row_off].reshape(3 * in_channels, out_channels)
            result = result + jnp.einsum(
                "fhwc,cd->fhwd", stacked, kernel, preferred_element_type=jnp.float32
            )
    return result


def attention_kernel(scale, q_ref, k_ref, v_ref, o_ref):
    scores = (
        jnp.dot(q_ref[0], k_ref[0], preferred_element_type=jnp.float32) * scale
    )
    largest = jnp.max(scores, axis=-1, keepdims=True)
    weights = jnp.exp(scores - largest)
    weight_sum = jnp.sum(weights, axis=-1, keepdims=True)
    summed = jnp.dot(weights.astype(v_ref.dtype), v_ref[0], preferred_element_type=jnp.float32)
    o_ref[0] = (summed / weight_sum).astype(o_ref.dtype)


def attend(queries, keys_all, values_all, scale):
    frames, count, channels = queries.shape
    tokens = keys_all.shape[2]
    flops = 4 * frames * count * tokens * channels
    moved = 2 * (queries.size * 2 + keys_all.size + values_all.size)
    return pl.pallas_call(
        functools.partial(attention_kernel, scale),
        grid=(frames,),
        in_specs=[
            pl.BlockSpec((1, count, channels), lambda f: (f, 0, 0)),
            pl.BlockSpec((1, channels, tokens), lambda f: (f, 0, 0)),
            pl.BlockSpec((1, tokens, channels), lambda f: (f, 0, 0)),
        ],
        out_specs=pl.BlockSpec((1, count, channels), lambda f: (f, 0, 0)),
        out_shape=jax.ShapeDtypeStruct(queries.shape, queries.dtype),
        compiler_params=pltpu.CompilerParams(vmem_limit_bytes=60 * 1024 * 1024),
        cost_estimate=pl.CostEstimate(
            flops=flops, transcendentals=frames * count * tokens, bytes_accessed=moved
        ),
    )(queries, keys_all, values_all)


def project_rows(tokens, weight):
    return jnp.einsum("ftc,cd->ftd", tokens, weight, preferred_element_type=jnp.float32).astype(
        jnp.bfloat16
    )


def per_device(
    features,
    first_cache,
    second_cache,
    w_query,
    w_key,
    w_value,
    w_output,
    w_first,
    w_upsample,
    w_second,
):
    frame_count, row_count, width_count, channels = features.shape
    core = lax.axis_index("ha") % 2
    count = lax.axis_size("ha")
    swap = [(i, i ^ 1) for i in range(count)]
    other = lax.dynamic_slice_in_dim(features, 1 - core, 1, axis=0)
    mine = lax.dynamic_slice_in_dim(features, core, 1, axis=0)
    block = jnp.concatenate([mine, lax.ppermute(other, "ha", swap)], axis=1)
    every_row = gather_chip_rows(block)
    normed_all = rms_scale(every_row).astype(jnp.bfloat16)
    all_tokens = normed_all.reshape(1, -1, channels)
    normed = rms_scale(block).astype(jnp.bfloat16)
    normed_tokens = normed.reshape(1, -1, channels)
    queries = project_rows(normed_tokens, w_query)
    keys_all = jnp.einsum(
        "ftc,cd->fdt", all_tokens, w_key, preferred_element_type=jnp.float32
    ).astype(jnp.bfloat16)
    values_all = project_rows(all_tokens, w_value)
    score_scale = 1.0 / math.sqrt(channels)
    attended = attend(queries, keys_all, values_all, score_scale)
    projected = jnp.einsum("ftc,cd->ftd", attended, w_output, preferred_element_type=jnp.float32)
    mixed_block = (block.astype(jnp.float32) + projected.reshape(block.shape)).astype(
        jnp.bfloat16
    )
    back = lax.ppermute(mixed_block[:, 1:2], "ha", swap)
    own = mixed_block[:, 0:1]
    mixed = jnp.where(
        core == 0,
        jnp.concatenate([own, back], axis=0),
        jnp.concatenate([back, own], axis=0),
    )
    first_in = jax.nn.silu(rms_scale(mixed)).astype(jnp.bfloat16)
    first_stack = jnp.concatenate([first_cache, first_in], axis=0)
    first_padded = extended(first_stack, 1, 1)
    block_out = (mixed.astype(jnp.float32) + conv_taps(first_padded, w_first, 3)).astype(
        jnp.bfloat16
    )
    block_padded = extended(block_out, 1, 1)
    widened = jnp.repeat(block_padded, 2, axis=2)
    upsampled = conv_taps(widened, w_upsample[None], 1, rows=((0, 1), (1, 1), (1, 2))).astype(
        jnp.bfloat16
    )
    second_in = jax.nn.silu(rms_scale(upsampled)).astype(jnp.bfloat16)
    second_stack = jnp.concatenate([second_cache, second_in], axis=0)
    second_padded = extended(second_stack, 1, 1)
    return (upsampled.astype(jnp.float32) + conv_taps(second_padded, w_second, 3)).astype(
        jnp.bfloat16
    )


def solution(mesh):
    placed = (
        P("grp", "ha", None, None),
        P("grp", "ha", None, None),
        P("grp", "ha", None, None),
        P(),
        P(),
        P(),
        P(),
        P(),
        P(),
        P(),
    )
    return jax.shard_map(
        per_device,
        mesh=mesh,
        in_specs=placed,
        out_specs=P("grp", "ha", None, None),
        check_vma=False,
    )
```

```python
import functools
import math

import jax
import jax.numpy as jnp
from jax import lax
from jax.experimental import pallas as pl
from jax.experimental.pallas import tpu as pltpu
from jax.sharding import PartitionSpec as P


def halo_rows(x, dim, width):
    count, length = (lax.axis_size("ha"), x.shape[dim])
    up = [(i, i + 1) for i in range(count - 1)]
    down = [(j, i) for i, j in up]
    last = lax.slice_in_dim(x, length - width, length, axis=dim)
    first = lax.slice_in_dim(x, 0, width, axis=dim)
    before = lax.ppermute(last, "ha", up)
    after = lax.ppermute(first, "ha", down)
    return before, after


def extended(x, dim, width):
    before, after = halo_rows(x, dim, width)
    return jnp.concatenate([before, x, after], axis=dim)


def gather_chip_rows(x):
    count = lax.axis_size("ha")
    chips = count // 2
    ring = list(range(0, chips, 2)) + list(range(chips - 1 - chips % 2, 0, -2))
    if chips % 2:
        ring = list(range(chips))
    place = {c: i for i, c in enumerate(ring)}

    def toward(step):
        return [
            (2 * c + k, 2 * ring[(place[c] + step) % chips] + k)
            for c in range(chips)
            for k in range(2)
        ]

    forward, backward = toward(1), toward(-1)
    pieces = [x]
    ahead = behind = x
    for step in range(1, chips // 2 + 1):
        ahead = lax.ppermute(ahead, "ha", forward)
        pieces.append(ahead)
        if step < chips - step:
            behind = lax.ppermute(behind, "ha", backward)
            pieces.append(behind)
    return jnp.concatenate(pieces, axis=1)


def gather_rows(x):
    count = lax.axis_size("ha")
    chips = count // 2
    pieces = [x]
    for shift in range(1, chips):
        pairs = [
            (2 * c + k, 2 * ((c + shift) % chips) + k) for c in range(chips) for k in range(2)
        ]
        pieces.append(lax.ppermute(x, "ha", pairs))
    own_chip = jnp.concatenate(pieces, axis=1)
    swap = [(2 * c + k, 2 * c + 1 - k) for c in range(chips) for k in range(2)]
    other = lax.ppermute(own_chip, "ha", swap)
    return jnp.concatenate([own_chip, other], axis=1)


def rms_scale(tensor):
    widened = tensor.astype(jnp.float32)
    return widened * lax.rsqrt(jnp.mean(widened * widened, axis=-1, keepdims=True) + 1e-06)


def conv_taps(padded, weight, time_taps, rows=None):
    frames_out = padded.shape[0] - time_taps + 1
    height_out = padded.shape[1] - 2 if rows is None else len(rows[0])
    width_out = padded.shape[2]
    in_channels = weight.shape[-2]
    out_channels = weight.shape[-1]
    widened = jnp.pad(padded, ((0, 0), (0, 0), (1, 1), (0, 0)))
    result = jnp.zeros((frames_out, height_out, width_out, out_channels), jnp.float32)
    for time_off in range(time_taps):
        for row_off in range(3):
            if rows is None:
                window = widened[time_off : time_off + frames_out, row_off : row_off + height_out]
            else:
                window = jnp.stack(
                    [widened[time_off : time_off + frames_out, r] for r in rows[row_off]], axis=1
                )
            stacked = jnp.concatenate(
                [window[:, :, col_off : col_off + width_out] for col_off in range(3)], axis=-1
            )
            kernel = weight[time_off, row_off].reshape(3 * in_channels, out_channels)
            result = result + jnp.einsum(
                "fhwc,cd->fhwd", stacked, kernel, preferred_element_type=jnp.float32
            )
    return result


def attention_kernel(scale, q_ref, k_ref, v_ref, o_ref):
    scores = (
        jnp.dot(q_ref[0], k_ref[0], preferred_element_type=jnp.float32) * scale
    )
    largest = jnp.max(scores, axis=-1, keepdims=True)
    weights = jnp.exp(scores - largest)
    weight_sum = jnp.sum(weights, axis=-1, keepdims=True)
    summed = jnp.dot(weights.astype(v_ref.dtype), v_ref[0], preferred_element_type=jnp.float32)
    o_ref[0] = (summed / weight_sum).astype(o_ref.dtype)


def attend(queries, keys_all, values_all, scale):
    frames, count, channels = queries.shape
    tokens = keys_all.shape[2]
    flops = 4 * frames * count * tokens * channels
    moved = 2 * (queries.size * 2 + keys_all.size + values_all.size)
    return pl.pallas_call(
        functools.partial(attention_kernel, scale),
        grid=(frames,),
        in_specs=[
            pl.BlockSpec((1, count, channels), lambda f: (f, 0, 0)),
            pl.BlockSpec((1, channels, tokens), lambda f: (f, 0, 0)),
            pl.BlockSpec((1, tokens, channels), lambda f: (f, 0, 0)),
        ],
        out_specs=pl.BlockSpec((1, count, channels), lambda f: (f, 0, 0)),
        out_shape=jax.ShapeDtypeStruct(queries.shape, queries.dtype),
        compiler_params=pltpu.CompilerParams(vmem_limit_bytes=60 * 1024 * 1024),
        cost_estimate=pl.CostEstimate(
            flops=flops, transcendentals=frames * count * tokens, bytes_accessed=moved
        ),
    )(queries, keys_all, values_all)


def project_rows(tokens, weight):
    return jnp.einsum("ftc,cd->ftd", tokens, weight, preferred_element_type=jnp.float32).astype(
        jnp.bfloat16
    )


def per_device(
    features,
    first_cache,
    second_cache,
    w_query,
    w_key,
    w_value,
    w_output,
    w_first,
    w_upsample,
    w_second,
):
    frame_count, row_count, width_count, channels = features.shape
    core = lax.axis_index("ha") % 2
    count = lax.axis_size("ha")
    swap = [(i, i ^ 1) for i in range(count)]
    other = lax.dynamic_slice_in_dim(features, 1 - core, 1, axis=0)
    mine = lax.dynamic_slice_in_dim(features, core, 1, axis=0)
    block = jnp.concatenate([mine, lax.ppermute(other, "ha", swap)], axis=1)
    every_row = gather_chip_rows(block)
    normed_all = rms_scale(every_row).astype(jnp.bfloat16)
    all_tokens = normed_all.reshape(1, -1, channels)
    normed = rms_scale(block).astype(jnp.bfloat16)
    normed_tokens = normed.reshape(1, -1, channels)
    queries = project_rows(normed_tokens, w_query)
    keys_all = jnp.einsum(
        "ftc,cd->fdt", all_tokens, w_key, preferred_element_type=jnp.float32
    ).astype(jnp.bfloat16)
    values_all = project_rows(all_tokens, w_value)
    score_scale = 1.0 / math.sqrt(channels)
    attended = attend(queries, keys_all, values_all, score_scale)
    projected = jnp.einsum("ftc,cd->ftd", attended, w_output, preferred_element_type=jnp.float32)
    mixed_block = (block.astype(jnp.float32) + projected.reshape(block.shape)).astype(
        jnp.bfloat16
    )
    back = lax.ppermute(mixed_block[:, 1:2], "ha", swap)
    own = mixed_block[:, 0:1]
    mixed = jnp.where(
        core == 0,
        jnp.concatenate([own, back], axis=0),
        jnp.concatenate([back, own], axis=0),
    )
    first_in = jax.nn.silu(rms_scale(mixed)).astype(jnp.bfloat16)
    first_stack = jnp.concatenate([first_cache, first_in], axis=0)
    first_padded = extended(first_stack, 1, 1)
    block_out = (mixed.astype(jnp.float32) + conv_taps(first_padded, w_first, 3)).astype(
        jnp.bfloat16
    )
    block_padded = extended(block_out, 1, 1)
    widened = jnp.repeat(block_padded, 2, axis=2)
    upsampled = conv_taps(widened, w_upsample[None], 1, rows=((0, 1), (1, 1), (1, 2))).astype(
        jnp.bfloat16
    )
    second_in = jax.nn.silu(rms_scale(upsampled)).astype(jnp.bfloat16)
    second_stack = jnp.concatenate([second_cache, second_in], axis=0)
    second_padded = extended(second_stack, 1, 1)
    return (upsampled.astype(jnp.float32) + conv_taps(second_padded, w_second, 3)).astype(
        jnp.bfloat16
    )


def solution(mesh):
    placed = (
        P("grp", "ha", None, None),
        P("grp", "ha", None, None),
        P("grp", "ha", None, None),
        P(),
        P(),
        P(),
        P(),
        P(),
        P(),
        P(),
    )
    return jax.shard_map(
        per_device,
        mesh=mesh,
        in_specs=placed,
        out_specs=P("grp", "ha", None, None),
        check_vma=False,
    )
```

```python
import functools
import math

import jax
import jax.numpy as jnp
from jax import lax
from jax.experimental import pallas as pl
from jax.experimental.pallas import tpu as pltpu
from jax.sharding import PartitionSpec as P


def halo_rows(x, dim, width):
    count, length = (lax.axis_size("ha"), x.shape[dim])
    up = [(i, i + 1) for i in range(count - 1)]
    down = [(j, i) for i, j in up]
    last = lax.slice_in_dim(x, length - width, length, axis=dim)
    first = lax.slice_in_dim(x, 0, width, axis=dim)
    before = lax.ppermute(last, "ha", up)
    after = lax.ppermute(first, "ha", down)
    return before, after


def extended(x, dim, width):
    before, after = halo_rows(x, dim, width)
    return jnp.concatenate([before, x, after], axis=dim)


def gather_chip_rows(x):
    count = lax.axis_size("ha")
    chips = count // 2
    ring = list(range(0, chips, 2)) + list(range(chips - 1 - chips % 2, 0, -2))
    if chips % 2:
        ring = list(range(chips))
    place = {c: i for i, c in enumerate(ring)}

    def toward(step):
        return [
            (2 * c + k, 2 * ring[(place[c] + step) % chips] + k)
            for c in range(chips)
            for k in range(2)
        ]

    forward, backward = toward(1), toward(-1)
    pieces = [x]
    ahead = behind = x
    for step in range(1, chips // 2 + 1):
        ahead = lax.ppermute(ahead, "ha", forward)
        pieces.append(ahead)
        if step < chips - step:
            behind = lax.ppermute(behind, "ha", backward)
            pieces.append(behind)
    return pieces


def gather_rows(x):
    count = lax.axis_size("ha")
    chips = count // 2
    pieces = [x]
    for shift in range(1, chips):
        pairs = [
            (2 * c + k, 2 * ((c + shift) % chips) + k) for c in range(chips) for k in range(2)
        ]
        pieces.append(lax.ppermute(x, "ha", pairs))
    own_chip = jnp.concatenate(pieces, axis=1)
    swap = [(2 * c + k, 2 * c + 1 - k) for c in range(chips) for k in range(2)]
    other = lax.ppermute(own_chip, "ha", swap)
    return jnp.concatenate([own_chip, other], axis=1)


def rms_scale(tensor):
    widened = tensor.astype(jnp.float32)
    return widened * lax.rsqrt(jnp.mean(widened * widened, axis=-1, keepdims=True) + 1e-06)


def conv_taps(padded, weight, time_taps, rows=None):
    frames_out = padded.shape[0] - time_taps + 1
    height_out = padded.shape[1] - 2 if rows is None else len(rows[0])
    width_out = padded.shape[2]
    in_channels = weight.shape[-2]
    out_channels = weight.shape[-1]
    widened = jnp.pad(padded, ((0, 0), (0, 0), (1, 1), (0, 0)))
    result = jnp.zeros((frames_out, height_out, width_out, out_channels), jnp.float32)
    for time_off in range(time_taps):
        for row_off in range(3):
            if rows is None:
                window = widened[time_off : time_off + frames_out, row_off : row_off + height_out]
            else:
                window = jnp.stack(
                    [widened[time_off : time_off + frames_out, r] for r in rows[row_off]], axis=1
                )
            stacked = jnp.concatenate(
                [window[:, :, col_off : col_off + width_out] for col_off in range(3)], axis=-1
            )
            kernel = weight[time_off, row_off].reshape(3 * in_channels, out_channels)
            result = result + jnp.einsum(
                "fhwc,cd->fhwd", stacked, kernel, preferred_element_type=jnp.float32
            )
    return result


def attention_kernel(scale, parts, q_ref, *refs):
    o_ref = refs[-1]
    key_refs, value_refs = refs[:parts], refs[parts : 2 * parts]
    query = q_ref[0]
    scores = [
        jnp.dot(query, k_ref[0], preferred_element_type=jnp.float32) * scale for k_ref in key_refs
    ]
    largest = scores[0].max(axis=-1, keepdims=True)
    for part in scores[1:]:
        largest = jnp.maximum(largest, part.max(axis=-1, keepdims=True))
    weight_sum = None
    summed = None
    for part, v_ref in zip(scores, value_refs):
        weights = jnp.exp(part - largest)
        part_sum = jnp.sum(weights, axis=-1, keepdims=True)
        product = jnp.dot(
            weights.astype(v_ref.dtype), v_ref[0], preferred_element_type=jnp.float32
        )
        weight_sum = part_sum if weight_sum is None else weight_sum + part_sum
        summed = product if summed is None else summed + product
    o_ref[0] = (summed / weight_sum).astype(o_ref.dtype)


def attend(queries, key_parts, value_parts, scale):
    frames, count, channels = queries.shape
    parts = len(key_parts)
    tokens = sum(k.shape[2] for k in key_parts)
    flops = 4 * frames * count * tokens * channels
    moved = 2 * (queries.size * 2 + 2 * tokens * channels * frames)
    specs = [pl.BlockSpec((1, count, channels), lambda f: (f, 0, 0))]
    specs += [pl.BlockSpec((1,) + k.shape[1:], lambda f: (f, 0, 0)) for k in key_parts]
    specs += [pl.BlockSpec((1,) + v.shape[1:], lambda f: (f, 0, 0)) for v in value_parts]
    return pl.pallas_call(
        functools.partial(attention_kernel, scale, parts),
        grid=(frames,),
        in_specs=specs,
        out_specs=pl.BlockSpec((1, count, channels), lambda f: (f, 0, 0)),
        out_shape=jax.ShapeDtypeStruct(queries.shape, queries.dtype),
        compiler_params=pltpu.CompilerParams(vmem_limit_bytes=60 * 1024 * 1024),
        cost_estimate=pl.CostEstimate(
            flops=flops, transcendentals=frames * count * tokens, bytes_accessed=moved
        ),
    )(queries, *key_parts, *value_parts)


def project_rows(tokens, weight):
    return jnp.einsum("ftc,cd->ftd", tokens, weight, preferred_element_type=jnp.float32).astype(
        jnp.bfloat16
    )


def per_device(
    features,
    first_cache,
    second_cache,
    w_query,
    w_key,
    w_value,
    w_output,
    w_first,
    w_upsample,
    w_second,
):
    frame_count, row_count, width_count, channels = features.shape
    core = lax.axis_index("ha") % 2
    count = lax.axis_size("ha")
    swap = [(i, i ^ 1) for i in range(count)]
    other = lax.dynamic_slice_in_dim(features, 1 - core, 1, axis=0)
    mine = lax.dynamic_slice_in_dim(features, core, 1, axis=0)
    block = jnp.concatenate([mine, lax.ppermute(other, "ha", swap)], axis=1)
    normed = rms_scale(block).astype(jnp.bfloat16)
    normed_tokens = normed.reshape(1, -1, channels)
    queries = project_rows(normed_tokens, w_query)
    key_parts, value_parts = [], []
    for piece in gather_chip_rows(block):
        piece_tokens = rms_scale(piece).astype(jnp.bfloat16).reshape(1, -1, channels)
        key_parts.append(
            jnp.einsum(
                "ftc,cd->fdt", piece_tokens, w_key, preferred_element_type=jnp.float32
            ).astype(jnp.bfloat16)
        )
        value_parts.append(project_rows(piece_tokens, w_value))
    score_scale = 1.0 / math.sqrt(channels)
    attended = attend(queries, key_parts, value_parts, score_scale)
    projected = jnp.einsum("ftc,cd->ftd", attended, w_output, preferred_element_type=jnp.float32)
    mixed_block = (block.astype(jnp.float32) + projected.reshape(block.shape)).astype(
        jnp.bfloat16
    )
    back = lax.ppermute(mixed_block[:, 1:2], "ha", swap)
    own = mixed_block[:, 0:1]
    mixed = jnp.where(
        core == 0,
        jnp.concatenate([own, back], axis=0),
        jnp.concatenate([back, own], axis=0),
    )
    first_in = jax.nn.silu(rms_scale(mixed)).astype(jnp.bfloat16)
    first_stack = jnp.concatenate([first_cache, first_in], axis=0)
    first_padded = extended(first_stack, 1, 1)
    block_out = (mixed.astype(jnp.float32) + conv_taps(first_padded, w_first, 3)).astype(
        jnp.bfloat16
    )
    block_padded = extended(block_out, 1, 1)
    widened = jnp.repeat(block_padded, 2, axis=2)
    upsampled = conv_taps(widened, w_upsample[None], 1, rows=((0, 1), (1, 1), (1, 2))).astype(
        jnp.bfloat16
    )
    second_in = jax.nn.silu(rms_scale(upsampled)).astype(jnp.bfloat16)
    second_stack = jnp.concatenate([second_cache, second_in], axis=0)
    second_padded = extended(second_stack, 1, 1)
    return (upsampled.astype(jnp.float32) + conv_taps(second_padded, w_second, 3)).astype(
        jnp.bfloat16
    )


def solution(mesh):
    placed = (
        P("grp", "ha", None, None),
        P("grp", "ha", None, None),
        P("grp", "ha", None, None),
        P(),
        P(),
        P(),
        P(),
        P(),
        P(),
        P(),
    )
    return jax.shard_map(
        per_device,
        mesh=mesh,
        in_specs=placed,
        out_specs=P("grp", "ha", None, None),
        check_vma=False,
    )
```

```python
import functools
import math

import jax
import jax.numpy as jnp
from jax import lax
from jax.experimental import pallas as pl
from jax.experimental.pallas import tpu as pltpu
from jax.sharding import PartitionSpec as P


def halo_rows(x, dim, width):
    count, length = (lax.axis_size("ha"), x.shape[dim])
    up = [(i, i + 1) for i in range(count - 1)]
    down = [(j, i) for i, j in up]
    last = lax.slice_in_dim(x, length - width, length, axis=dim)
    first = lax.slice_in_dim(x, 0, width, axis=dim)
    before = lax.ppermute(last, "ha", up)
    after = lax.ppermute(first, "ha", down)
    return before, after


def extended(x, dim, width):
    before, after = halo_rows(x, dim, width)
    return jnp.concatenate([before, x, after], axis=dim)


def gather_chip_rows(x):
    count = lax.axis_size("ha")
    chips = count // 2
    ring = list(range(0, chips, 2)) + list(range(chips - 1 - chips % 2, 0, -2))
    if chips % 2:
        ring = list(range(chips))
    place = {c: i for i, c in enumerate(ring)}

    def toward(step):
        return [
            (2 * c + k, 2 * ring[(place[c] + step) % chips] + k)
            for c in range(chips)
            for k in range(2)
        ]

    forward, backward = toward(1), toward(-1)
    pieces = [x]
    ahead = behind = x
    for step in range(1, chips // 2 + 1):
        ahead = lax.ppermute(ahead, "ha", forward)
        pieces.append(ahead)
        if step < chips - step:
            behind = lax.ppermute(behind, "ha", backward)
            pieces.append(behind)
    return jnp.concatenate(pieces, axis=1)


def gather_rows(x):
    count = lax.axis_size("ha")
    chips = count // 2
    pieces = [x]
    for shift in range(1, chips):
        pairs = [
            (2 * c + k, 2 * ((c + shift) % chips) + k) for c in range(chips) for k in range(2)
        ]
        pieces.append(lax.ppermute(x, "ha", pairs))
    own_chip = jnp.concatenate(pieces, axis=1)
    swap = [(2 * c + k, 2 * c + 1 - k) for c in range(chips) for k in range(2)]
    other = lax.ppermute(own_chip, "ha", swap)
    return jnp.concatenate([own_chip, other], axis=1)


def rms_scale(tensor):
    widened = tensor.astype(jnp.float32)
    return widened * lax.rsqrt(jnp.mean(widened * widened, axis=-1, keepdims=True) + 1e-06)


def conv_taps(padded, weight, time_taps, rows=None):
    frames_out = padded.shape[0] - time_taps + 1
    height_out = padded.shape[1] - 2 if rows is None else len(rows[0])
    width_out = padded.shape[2]
    in_channels = weight.shape[-2]
    out_channels = weight.shape[-1]
    widened = jnp.pad(padded, ((0, 0), (0, 0), (1, 1), (0, 0)))
    result = jnp.zeros((frames_out, height_out, width_out, out_channels), jnp.float32)
    for time_off in range(time_taps):
        for row_off in range(3):
            if rows is None:
                window = widened[time_off : time_off + frames_out, row_off : row_off + height_out]
            else:
                window = jnp.stack(
                    [widened[time_off : time_off + frames_out, r] for r in rows[row_off]], axis=1
                )
            stacked = jnp.concatenate(
                [window[:, :, col_off : col_off + width_out] for col_off in range(3)], axis=-1
            )
            kernel = weight[time_off, row_off].reshape(3 * in_channels, out_channels)
            result = result + jnp.einsum(
                "fhwc,cd->fhwd", stacked, kernel, preferred_element_type=jnp.float32
            )
    return result


def attention_kernel(scale, q_ref, n_ref, wk_ref, wv_ref, o_ref):
    tokens = n_ref[0]
    keys = jnp.dot(tokens, wk_ref[...], preferred_element_type=jnp.float32).astype(tokens.dtype)
    values = jnp.dot(tokens, wv_ref[...], preferred_element_type=jnp.float32).astype(tokens.dtype)
    scores = (
        lax.dot_general(
            q_ref[0], keys, (((1,), (1,)), ((), ())), preferred_element_type=jnp.float32
        )
        * scale
    )
    largest = jnp.max(scores, axis=-1, keepdims=True)
    weights = jnp.exp(scores - largest)
    weight_sum = jnp.sum(weights, axis=-1, keepdims=True)
    summed = jnp.dot(weights.astype(values.dtype), values, preferred_element_type=jnp.float32)
    o_ref[0] = (summed / weight_sum).astype(o_ref.dtype)


def attend(queries, all_tokens, w_key, w_value, scale):
    frames, count, channels = queries.shape
    tokens = all_tokens.shape[1]
    flops = 4 * frames * count * tokens * channels + 4 * frames * tokens * channels * channels
    moved = 2 * (queries.size * 2 + all_tokens.size + w_key.size + w_value.size)
    return pl.pallas_call(
        functools.partial(attention_kernel, scale),
        grid=(frames,),
        in_specs=[
            pl.BlockSpec((1, count, channels), lambda f: (f, 0, 0)),
            pl.BlockSpec((1, tokens, channels), lambda f: (f, 0, 0)),
            pl.BlockSpec(w_key.shape, lambda f: (0, 0)),
            pl.BlockSpec(w_value.shape, lambda f: (0, 0)),
        ],
        out_specs=pl.BlockSpec((1, count, channels), lambda f: (f, 0, 0)),
        out_shape=jax.ShapeDtypeStruct(queries.shape, queries.dtype),
        compiler_params=pltpu.CompilerParams(vmem_limit_bytes=60 * 1024 * 1024),
        cost_estimate=pl.CostEstimate(
            flops=flops, transcendentals=frames * count * tokens, bytes_accessed=moved
        ),
    )(queries, all_tokens, w_key, w_value)


def project_rows(tokens, weight):
    return jnp.einsum("ftc,cd->ftd", tokens, weight, preferred_element_type=jnp.float32).astype(
        jnp.bfloat16
    )


def per_device(
    features,
    first_cache,
    second_cache,
    w_query,
    w_key,
    w_value,
    w_output,
    w_first,
    w_upsample,
    w_second,
):
    frame_count, row_count, width_count, channels = features.shape
    core = lax.axis_index("ha") % 2
    count = lax.axis_size("ha")
    swap = [(i, i ^ 1) for i in range(count)]
    other = lax.dynamic_slice_in_dim(features, 1 - core, 1, axis=0)
    mine = lax.dynamic_slice_in_dim(features, core, 1, axis=0)
    block = jnp.concatenate([mine, lax.ppermute(other, "ha", swap)], axis=1)
    every_row = gather_chip_rows(block)
    normed_all = rms_scale(every_row).astype(jnp.bfloat16)
    all_tokens = normed_all.reshape(1, -1, channels)
    normed = rms_scale(block).astype(jnp.bfloat16)
    normed_tokens = normed.reshape(1, -1, channels)
    queries = project_rows(normed_tokens, w_query)
    score_scale = 1.0 / math.sqrt(channels)
    attended = attend(queries, all_tokens, w_key, w_value, score_scale)
    projected = jnp.einsum("ftc,cd->ftd", attended, w_output, preferred_element_type=jnp.float32)
    mixed_block = (block.astype(jnp.float32) + projected.reshape(block.shape)).astype(
        jnp.bfloat16
    )
    back = lax.ppermute(mixed_block[:, 1:2], "ha", swap)
    own = mixed_block[:, 0:1]
    mixed = jnp.where(
        core == 0,
        jnp.concatenate([own, back], axis=0),
        jnp.concatenate([back, own], axis=0),
    )
    first_in = jax.nn.silu(rms_scale(mixed)).astype(jnp.bfloat16)
    first_stack = jnp.concatenate([first_cache, first_in], axis=0)
    first_padded = extended(first_stack, 1, 1)
    block_out = (mixed.astype(jnp.float32) + conv_taps(first_padded, w_first, 3)).astype(
        jnp.bfloat16
    )
    block_padded = extended(block_out, 1, 1)
    widened = jnp.repeat(block_padded, 2, axis=2)
    upsampled = conv_taps(widened, w_upsample[None], 1, rows=((0, 1), (1, 1), (1, 2))).astype(
        jnp.bfloat16
    )
    second_in = jax.nn.silu(rms_scale(upsampled)).astype(jnp.bfloat16)
    second_stack = jnp.concatenate([second_cache, second_in], axis=0)
    second_padded = extended(second_stack, 1, 1)
    return (upsampled.astype(jnp.float32) + conv_taps(second_padded, w_second, 3)).astype(
        jnp.bfloat16
    )


def solution(mesh):
    placed = (
        P("grp", "ha", None, None),
        P("grp", "ha", None, None),
        P("grp", "ha", None, None),
        P(),
        P(),
        P(),
        P(),
        P(),
        P(),
        P(),
    )
    return jax.shard_map(
        per_device,
        mesh=mesh,
        in_specs=placed,
        out_specs=P("grp", "ha", None, None),
        check_vma=False,
    )
```

```python
import functools
import math

import jax
import jax.numpy as jnp
from jax import lax
from jax.experimental import pallas as pl
from jax.experimental.pallas import tpu as pltpu
from jax.sharding import PartitionSpec as P


def halo_rows(x, dim, width):
    count, length = (lax.axis_size("ha"), x.shape[dim])
    up = [(i, i + 1) for i in range(count - 1)]
    down = [(j, i) for i, j in up]
    last = lax.slice_in_dim(x, length - width, length, axis=dim)
    first = lax.slice_in_dim(x, 0, width, axis=dim)
    before = lax.ppermute(last, "ha", up)
    after = lax.ppermute(first, "ha", down)
    return before, after


def extended(x, dim, width):
    before, after = halo_rows(x, dim, width)
    return jnp.concatenate([before, x, after], axis=dim)


def gather_chip_rows(x):
    count = lax.axis_size("ha")
    chips = count // 2
    ring = list(range(0, chips, 2)) + list(range(chips - 1 - chips % 2, 0, -2))
    if chips % 2:
        ring = list(range(chips))
    place = {c: i for i, c in enumerate(ring)}

    def toward(step):
        return [
            (2 * c + k, 2 * ring[(place[c] + step) % chips] + k)
            for c in range(chips)
            for k in range(2)
        ]

    forward, backward = toward(1), toward(-1)
    pieces = [x]
    ahead = behind = x
    for step in range(1, chips // 2 + 1):
        ahead = lax.ppermute(ahead, "ha", forward)
        pieces.append(ahead)
        if step < chips - step:
            behind = lax.ppermute(behind, "ha", backward)
            pieces.append(behind)
    return jnp.concatenate(pieces, axis=1)


def gather_rows(x):
    count = lax.axis_size("ha")
    chips = count // 2
    pieces = [x]
    for shift in range(1, chips):
        pairs = [
            (2 * c + k, 2 * ((c + shift) % chips) + k) for c in range(chips) for k in range(2)
        ]
        pieces.append(lax.ppermute(x, "ha", pairs))
    own_chip = jnp.concatenate(pieces, axis=1)
    swap = [(2 * c + k, 2 * c + 1 - k) for c in range(chips) for k in range(2)]
    other = lax.ppermute(own_chip, "ha", swap)
    return jnp.concatenate([own_chip, other], axis=1)


def rms_scale(tensor):
    widened = tensor.astype(jnp.float32)
    return widened * lax.rsqrt(jnp.mean(widened * widened, axis=-1, keepdims=True) + 1e-06)


def conv_taps(padded, weight, time_taps, rows=None):
    frames_out = padded.shape[0] - time_taps + 1
    height_out = padded.shape[1] - 2 if rows is None else len(rows[0])
    width_out = padded.shape[2]
    in_channels = weight.shape[-2]
    out_channels = weight.shape[-1]
    widened = jnp.pad(padded, ((0, 0), (0, 0), (1, 1), (0, 0)))
    result = jnp.zeros((frames_out, height_out, width_out, out_channels), jnp.float32)
    for time_off in range(time_taps):
        for row_off in range(3):
            if rows is None:
                window = widened[time_off : time_off + frames_out, row_off : row_off + height_out]
            else:
                window = jnp.stack(
                    [widened[time_off : time_off + frames_out, r] for r in rows[row_off]], axis=1
                )
            stacked = jnp.concatenate(
                [window[:, :, col_off : col_off + width_out] for col_off in range(3)], axis=-1
            )
            kernel = weight[time_off, row_off].reshape(3 * in_channels, out_channels)
            result = result + jnp.einsum(
                "fhwc,cd->fhwd", stacked, kernel, preferred_element_type=jnp.float32
            )
    return result


def attention_kernel(scale, q_ref, x_ref, wk_ref, wv_ref, r_ref, wo_ref, o_ref):
    raw = x_ref[0].astype(jnp.float32)
    tokens = (raw * lax.rsqrt(jnp.mean(raw * raw, axis=-1, keepdims=True) + 1e-06)).astype(
        x_ref.dtype
    )
    keys = jnp.dot(tokens, wk_ref[...], preferred_element_type=jnp.float32).astype(tokens.dtype)
    values = jnp.dot(tokens, wv_ref[...], preferred_element_type=jnp.float32).astype(tokens.dtype)
    scores = (
        lax.dot_general(
            q_ref[0], keys, (((1,), (1,)), ((), ())), preferred_element_type=jnp.float32
        )
        * scale
    )
    largest = jnp.max(scores, axis=-1, keepdims=True)
    weights = jnp.exp(scores - largest)
    weight_sum = jnp.sum(weights, axis=-1, keepdims=True)
    summed = jnp.dot(weights.astype(values.dtype), values, preferred_element_type=jnp.float32)
    attended = (summed / weight_sum).astype(values.dtype)
    projected = jnp.dot(attended, wo_ref[...], preferred_element_type=jnp.float32)
    o_ref[0] = (r_ref[0].astype(jnp.float32) + projected).astype(o_ref.dtype)


def attend(queries, all_rows, w_key, w_value, residual, w_output, scale):
    frames, count, channels = queries.shape
    tokens = all_rows.shape[1]
    flops = 4 * frames * count * tokens * channels + 4 * frames * tokens * channels * channels
    moved = 2 * (queries.size * 3 + all_rows.size + 3 * w_key.size)
    return pl.pallas_call(
        functools.partial(attention_kernel, scale),
        grid=(frames,),
        in_specs=[
            pl.BlockSpec((1, count, channels), lambda f: (f, 0, 0)),
            pl.BlockSpec((1, tokens, channels), lambda f: (f, 0, 0)),
            pl.BlockSpec(w_key.shape, lambda f: (0, 0)),
            pl.BlockSpec(w_value.shape, lambda f: (0, 0)),
            pl.BlockSpec((1, count, channels), lambda f: (f, 0, 0)),
            pl.BlockSpec(w_output.shape, lambda f: (0, 0)),
        ],
        out_specs=pl.BlockSpec((1, count, channels), lambda f: (f, 0, 0)),
        out_shape=jax.ShapeDtypeStruct(queries.shape, queries.dtype),
        compiler_params=pltpu.CompilerParams(vmem_limit_bytes=60 * 1024 * 1024),
        cost_estimate=pl.CostEstimate(
            flops=flops, transcendentals=frames * count * tokens, bytes_accessed=moved
        ),
    )(queries, all_rows, w_key, w_value, residual, w_output)


def project_rows(tokens, weight):
    return jnp.einsum("ftc,cd->ftd", tokens, weight, preferred_element_type=jnp.float32).astype(
        jnp.bfloat16
    )


def per_device(
    features,
    first_cache,
    second_cache,
    w_query,
    w_key,
    w_value,
    w_output,
    w_first,
    w_upsample,
    w_second,
):
    frame_count, row_count, width_count, channels = features.shape
    core = lax.axis_index("ha") % 2
    count = lax.axis_size("ha")
    swap = [(i, i ^ 1) for i in range(count)]
    other = lax.dynamic_slice_in_dim(features, 1 - core, 1, axis=0)
    mine = lax.dynamic_slice_in_dim(features, core, 1, axis=0)
    block = jnp.concatenate([mine, lax.ppermute(other, "ha", swap)], axis=1)
    every_row = gather_chip_rows(block)
    all_rows = every_row.reshape(1, -1, channels)
    normed = rms_scale(block).astype(jnp.bfloat16)
    normed_tokens = normed.reshape(1, -1, channels)
    queries = project_rows(normed_tokens, w_query)
    score_scale = 1.0 / math.sqrt(channels)
    mixed_block = attend(
        queries,
        all_rows,
        w_key,
        w_value,
        block.reshape(queries.shape),
        w_output,
        score_scale,
    ).reshape(block.shape)
    back = lax.ppermute(mixed_block[:, 1:2], "ha", swap)
    own = mixed_block[:, 0:1]
    mixed = jnp.where(
        core == 0,
        jnp.concatenate([own, back], axis=0),
        jnp.concatenate([back, own], axis=0),
    )
    first_in = jax.nn.silu(rms_scale(mixed)).astype(jnp.bfloat16)
    first_stack = jnp.concatenate([first_cache, first_in], axis=0)
    first_padded = extended(first_stack, 1, 1)
    block_out = (mixed.astype(jnp.float32) + conv_taps(first_padded, w_first, 3)).astype(
        jnp.bfloat16
    )
    block_padded = extended(block_out, 1, 1)
    widened = jnp.repeat(block_padded, 2, axis=2)
    upsampled = conv_taps(widened, w_upsample[None], 1, rows=((0, 1), (1, 1), (1, 2))).astype(
        jnp.bfloat16
    )
    second_in = jax.nn.silu(rms_scale(upsampled)).astype(jnp.bfloat16)
    second_stack = jnp.concatenate([second_cache, second_in], axis=0)
    second_padded = extended(second_stack, 1, 1)
    return (upsampled.astype(jnp.float32) + conv_taps(second_padded, w_second, 3)).astype(
        jnp.bfloat16
    )


def solution(mesh):
    placed = (
        P("grp", "ha", None, None),
        P("grp", "ha", None, None),
        P("grp", "ha", None, None),
        P(),
        P(),
        P(),
        P(),
        P(),
        P(),
        P(),
    )
    return jax.shard_map(
        per_device,
        mesh=mesh,
        in_specs=placed,
        out_specs=P("grp", "ha", None, None),
        check_vma=False,
    )
```

```python
import functools
import math

import jax
import jax.numpy as jnp
from jax import lax
from jax.experimental import pallas as pl
from jax.experimental.pallas import tpu as pltpu
from jax.sharding import PartitionSpec as P


def halo_rows(x, dim, width):
    count, length = (lax.axis_size("ha"), x.shape[dim])
    up = [(i, i + 1) for i in range(count - 1)]
    down = [(j, i) for i, j in up]
    last = lax.slice_in_dim(x, length - width, length, axis=dim)
    first = lax.slice_in_dim(x, 0, width, axis=dim)
    before = lax.ppermute(last, "ha", up)
    after = lax.ppermute(first, "ha", down)
    return before, after


def extended(x, dim, width):
    before, after = halo_rows(x, dim, width)
    return jnp.concatenate([before, x, after], axis=dim)


def gather_chip_rows(x):
    count = lax.axis_size("ha")
    chips = count // 2
    ring = list(range(0, chips, 2)) + list(range(chips - 1 - chips % 2, 0, -2))
    if chips % 2:
        ring = list(range(chips))
    place = {c: i for i, c in enumerate(ring)}

    def toward(step):
        return [
            (2 * c + k, 2 * ring[(place[c] + step) % chips] + k)
            for c in range(chips)
            for k in range(2)
        ]

    forward, backward = toward(1), toward(-1)
    pieces = [x]
    ahead = behind = x
    for step in range(1, chips // 2 + 1):
        ahead = lax.ppermute(ahead, "ha", forward)
        pieces.append(ahead)
        if step < chips - step:
            behind = lax.ppermute(behind, "ha", backward)
            pieces.append(behind)
    return jnp.concatenate(pieces, axis=1)


def gather_rows(x):
    count = lax.axis_size("ha")
    chips = count // 2
    pieces = [x]
    for shift in range(1, chips):
        pairs = [
            (2 * c + k, 2 * ((c + shift) % chips) + k) for c in range(chips) for k in range(2)
        ]
        pieces.append(lax.ppermute(x, "ha", pairs))
    own_chip = jnp.concatenate(pieces, axis=1)
    swap = [(2 * c + k, 2 * c + 1 - k) for c in range(chips) for k in range(2)]
    other = lax.ppermute(own_chip, "ha", swap)
    return jnp.concatenate([own_chip, other], axis=1)


def rms_scale(tensor):
    widened = tensor.astype(jnp.float32)
    return widened * lax.rsqrt(jnp.mean(widened * widened, axis=-1, keepdims=True) + 1e-06)


def conv_taps(padded, weight, time_taps, rows=None):
    frames_out = padded.shape[0] - time_taps + 1
    height_out = padded.shape[1] - 2 if rows is None else len(rows[0])
    width_out = padded.shape[2]
    in_channels = weight.shape[-2]
    out_channels = weight.shape[-1]
    widened = jnp.pad(padded, ((0, 0), (0, 0), (1, 1), (0, 0)))
    result = jnp.zeros((frames_out, height_out, width_out, out_channels), jnp.float32)
    for time_off in range(time_taps):
        for row_off in range(3):
            if rows is None:
                window = widened[time_off : time_off + frames_out, row_off : row_off + height_out]
            else:
                window = jnp.stack(
                    [widened[time_off : time_off + frames_out, r] for r in rows[row_off]], axis=1
                )
            stacked = jnp.concatenate(
                [window[:, :, col_off : col_off + width_out] for col_off in range(3)], axis=-1
            )
            kernel = weight[time_off, row_off].reshape(3 * in_channels, out_channels)
            result = result + jnp.einsum(
                "fhwc,cd->fhwd", stacked, kernel, preferred_element_type=jnp.float32
            )
    return result


def attention_kernel(scale, q_ref, x_ref, wk_ref, wv_ref, r_ref, wo_ref, o_ref):
    raw = x_ref[0].astype(jnp.float32)
    tokens = (raw * lax.rsqrt(jnp.mean(raw * raw, axis=-1, keepdims=True) + 1e-06)).astype(
        x_ref.dtype
    )
    keys = jnp.dot(tokens, wk_ref[...], preferred_element_type=jnp.float32).astype(tokens.dtype)
    values = jnp.dot(tokens, wv_ref[...], preferred_element_type=jnp.float32).astype(tokens.dtype)
    scores = (
        lax.dot_general(
            q_ref[0], keys, (((1,), (1,)), ((), ())), preferred_element_type=jnp.float32
        )
        * scale
    )
    largest = jnp.max(scores, axis=-1, keepdims=True)
    weights = jnp.exp(scores - largest)
    weight_sum = jnp.sum(weights, axis=-1, keepdims=True)
    summed = jnp.dot(weights.astype(values.dtype), values, preferred_element_type=jnp.float32)
    attended = (summed / weight_sum).astype(values.dtype)
    projected = jnp.dot(attended, wo_ref[...], preferred_element_type=jnp.float32)
    o_ref[0] = (r_ref[0].astype(jnp.float32) + projected).astype(o_ref.dtype)


def attend(queries, all_rows, w_key, w_value, residual, w_output, scale):
    frames, count, channels = queries.shape
    tokens = all_rows.shape[1]
    flops = 4 * frames * count * tokens * channels + 4 * frames * tokens * channels * channels
    moved = 2 * (queries.size * 3 + all_rows.size + 3 * w_key.size)
    return pl.pallas_call(
        functools.partial(attention_kernel, scale),
        grid=(frames,),
        in_specs=[
            pl.BlockSpec((1, count, channels), lambda f: (f, 0, 0)),
            pl.BlockSpec((1, tokens, channels), lambda f: (f, 0, 0)),
            pl.BlockSpec(w_key.shape, lambda f: (0, 0)),
            pl.BlockSpec(w_value.shape, lambda f: (0, 0)),
            pl.BlockSpec((1, count, channels), lambda f: (f, 0, 0)),
            pl.BlockSpec(w_output.shape, lambda f: (0, 0)),
        ],
        out_specs=pl.BlockSpec((1, count, channels), lambda f: (f, 0, 0)),
        out_shape=jax.ShapeDtypeStruct(queries.shape, queries.dtype),
        compiler_params=pltpu.CompilerParams(vmem_limit_bytes=60 * 1024 * 1024),
        cost_estimate=pl.CostEstimate(
            flops=flops, transcendentals=frames * count * tokens, bytes_accessed=moved
        ),
    )(queries, all_rows, w_key, w_value, residual, w_output)


def conv_frames(padded, weight):
    frames, height, width, channels = padded.shape
    cols = jnp.pad(padded, ((0, 0), (0, 0), (1, 1), (0, 0)))
    result = None
    for row_off in range(3):
        window = cols[:, row_off : row_off + height - 2]
        stacked = jnp.concatenate([window[:, :, c : c + width] for c in range(3)], axis=-1)
        kernel = weight[row_off].reshape(3 * channels, weight.shape[-1])
        term = jnp.einsum("fhwc,cd->fhwd", stacked, kernel, preferred_element_type=jnp.float32)
        result = term if result is None else result + term
    return result


def cached_terms(cache_pad, weight):
    late = conv_frames(cache_pad[1:2], weight[1])
    return conv_frames(cache_pad, weight[0]) + jnp.concatenate(
        [late, jnp.zeros_like(late)], axis=0
    )


def new_terms(new_pad, weight):
    early = conv_frames(new_pad[0:1], weight[1])
    return conv_frames(new_pad, weight[2]) + jnp.concatenate(
        [jnp.zeros_like(early), early], axis=0
    )


def project_rows(tokens, weight):
    return jnp.einsum("ftc,cd->ftd", tokens, weight, preferred_element_type=jnp.float32).astype(
        jnp.bfloat16
    )


def per_device(
    features,
    first_cache,
    second_cache,
    w_query,
    w_key,
    w_value,
    w_output,
    w_first,
    w_upsample,
    w_second,
):
    frame_count, row_count, width_count, channels = features.shape
    first_cached = cached_terms(extended(first_cache, 1, 1), w_first)
    second_cached = cached_terms(extended(second_cache, 1, 1), w_second)
    core = lax.axis_index("ha") % 2
    count = lax.axis_size("ha")
    swap = [(i, i ^ 1) for i in range(count)]
    other = lax.dynamic_slice_in_dim(features, 1 - core, 1, axis=0)
    mine = lax.dynamic_slice_in_dim(features, core, 1, axis=0)
    block = jnp.concatenate([mine, lax.ppermute(other, "ha", swap)], axis=1)
    every_row = gather_chip_rows(block)
    all_rows = every_row.reshape(1, -1, channels)
    normed = rms_scale(block).astype(jnp.bfloat16)
    normed_tokens = normed.reshape(1, -1, channels)
    queries = project_rows(normed_tokens, w_query)
    score_scale = 1.0 / math.sqrt(channels)
    mixed_block = attend(
        queries,
        all_rows,
        w_key,
        w_value,
        block.reshape(queries.shape),
        w_output,
        score_scale,
    ).reshape(block.shape)
    back = lax.ppermute(mixed_block[:, 1:2], "ha", swap)
    own = mixed_block[:, 0:1]
    mixed = jnp.where(
        core == 0,
        jnp.concatenate([own, back], axis=0),
        jnp.concatenate([back, own], axis=0),
    )
    first_in = jax.nn.silu(rms_scale(mixed)).astype(jnp.bfloat16)
    first_new = new_terms(extended(first_in, 1, 1), w_first)
    block_out = (mixed.astype(jnp.float32) + first_cached + first_new).astype(jnp.bfloat16)
    block_padded = extended(block_out, 1, 1)
    widened = jnp.repeat(block_padded, 2, axis=2)
    upsampled = conv_taps(widened, w_upsample[None], 1, rows=((0, 1), (1, 1), (1, 2))).astype(
        jnp.bfloat16
    )
    second_in = jax.nn.silu(rms_scale(upsampled)).astype(jnp.bfloat16)
    second_new = new_terms(extended(second_in, 1, 1), w_second)
    return (upsampled.astype(jnp.float32) + second_cached + second_new).astype(jnp.bfloat16)


def solution(mesh):
    placed = (
        P("grp", "ha", None, None),
        P("grp", "ha", None, None),
        P("grp", "ha", None, None),
        P(),
        P(),
        P(),
        P(),
        P(),
        P(),
        P(),
    )
    return jax.shard_map(
        per_device,
        mesh=mesh,
        in_specs=placed,
        out_specs=P("grp", "ha", None, None),
        check_vma=False,
    )
```

```python
import functools
import math

import jax
import jax.numpy as jnp
from jax import lax
from jax.experimental import pallas as pl
from jax.experimental.pallas import tpu as pltpu
from jax.sharding import PartitionSpec as P


def halo_rows(x, dim, width):
    count, length = (lax.axis_size("ha"), x.shape[dim])
    up = [(i, i + 1) for i in range(count - 1)]
    down = [(j, i) for i, j in up]
    last = lax.slice_in_dim(x, length - width, length, axis=dim)
    first = lax.slice_in_dim(x, 0, width, axis=dim)
    before = lax.ppermute(last, "ha", up)
    after = lax.ppermute(first, "ha", down)
    return before, after


def extended(x, dim, width):
    before, after = halo_rows(x, dim, width)
    return jnp.concatenate([before, x, after], axis=dim)


def gather_chip_rows(x):
    count = lax.axis_size("ha")
    chips = count // 2
    ring = list(range(0, chips, 2)) + list(range(chips - 1 - chips % 2, 0, -2))
    if chips % 2:
        ring = list(range(chips))
    place = {c: i for i, c in enumerate(ring)}

    def toward(step):
        return [
            (2 * c + k, 2 * ring[(place[c] + step) % chips] + k)
            for c in range(chips)
            for k in range(2)
        ]

    forward, backward = toward(1), toward(-1)
    pieces = [x]
    ahead = behind = x
    for step in range(1, chips // 2 + 1):
        if step == chips - step and x.shape[1] > 1:
            half = x.shape[1] // 2
            first = lax.ppermute(ahead[:, :half], "ha", forward)
            second = lax.ppermute(behind[:, half:], "ha", backward)
            pieces.append(jnp.concatenate([first, second], axis=1))
            continue
        ahead = lax.ppermute(ahead, "ha", forward)
        pieces.append(ahead)
        if step < chips - step:
            behind = lax.ppermute(behind, "ha", backward)
            pieces.append(behind)
    return jnp.concatenate(pieces, axis=1)


def gather_rows(x):
    count = lax.axis_size("ha")
    chips = count // 2
    pieces = [x]
    for shift in range(1, chips):
        pairs = [
            (2 * c + k, 2 * ((c + shift) % chips) + k) for c in range(chips) for k in range(2)
        ]
        pieces.append(lax.ppermute(x, "ha", pairs))
    own_chip = jnp.concatenate(pieces, axis=1)
    swap = [(2 * c + k, 2 * c + 1 - k) for c in range(chips) for k in range(2)]
    other = lax.ppermute(own_chip, "ha", swap)
    return jnp.concatenate([own_chip, other], axis=1)


def rms_scale(tensor):
    widened = tensor.astype(jnp.float32)
    return widened * lax.rsqrt(jnp.mean(widened * widened, axis=-1, keepdims=True) + 1e-06)


def conv_taps(padded, weight, time_taps, rows=None):
    frames_out = padded.shape[0] - time_taps + 1
    height_out = padded.shape[1] - 2 if rows is None else len(rows[0])
    width_out = padded.shape[2]
    in_channels = weight.shape[-2]
    out_channels = weight.shape[-1]
    widened = jnp.pad(padded, ((0, 0), (0, 0), (1, 1), (0, 0)))
    result = jnp.zeros((frames_out, height_out, width_out, out_channels), jnp.float32)
    for time_off in range(time_taps):
        for row_off in range(3):
            if rows is None:
                window = widened[time_off : time_off + frames_out, row_off : row_off + height_out]
            else:
                window = jnp.stack(
                    [widened[time_off : time_off + frames_out, r] for r in rows[row_off]], axis=1
                )
            stacked = jnp.concatenate(
                [window[:, :, col_off : col_off + width_out] for col_off in range(3)], axis=-1
            )
            kernel = weight[time_off, row_off].reshape(3 * in_channels, out_channels)
            result = result + jnp.einsum(
                "fhwc,cd->fhwd", stacked, kernel, preferred_element_type=jnp.float32
            )
    return result


def attention_kernel(scale, q_ref, x_ref, wk_ref, wv_ref, r_ref, wo_ref, o_ref):
    raw = x_ref[0].astype(jnp.float32)
    tokens = (raw * lax.rsqrt(jnp.mean(raw * raw, axis=-1, keepdims=True) + 1e-06)).astype(
        x_ref.dtype
    )
    keys = jnp.dot(tokens, wk_ref[...], preferred_element_type=jnp.float32).astype(tokens.dtype)
    values = jnp.dot(tokens, wv_ref[...], preferred_element_type=jnp.float32).astype(tokens.dtype)
    scores = (
        lax.dot_general(
            q_ref[0], keys, (((1,), (1,)), ((), ())), preferred_element_type=jnp.float32
        )
        * scale
    )
    largest = jnp.max(scores, axis=-1, keepdims=True)
    weights = jnp.exp(scores - largest)
    weight_sum = jnp.sum(weights, axis=-1, keepdims=True)
    summed = jnp.dot(weights.astype(values.dtype), values, preferred_element_type=jnp.float32)
    attended = (summed / weight_sum).astype(values.dtype)
    projected = jnp.dot(attended, wo_ref[...], preferred_element_type=jnp.float32)
    o_ref[0] = (r_ref[0].astype(jnp.float32) + projected).astype(o_ref.dtype)


def attend(queries, all_rows, w_key, w_value, residual, w_output, scale):
    frames, count, channels = queries.shape
    tokens = all_rows.shape[1]
    flops = 4 * frames * count * tokens * channels + 4 * frames * tokens * channels * channels
    moved = 2 * (queries.size * 3 + all_rows.size + 3 * w_key.size)
    return pl.pallas_call(
        functools.partial(attention_kernel, scale),
        grid=(frames,),
        in_specs=[
            pl.BlockSpec((1, count, channels), lambda f: (f, 0, 0)),
            pl.BlockSpec((1, tokens, channels), lambda f: (f, 0, 0)),
            pl.BlockSpec(w_key.shape, lambda f: (0, 0)),
            pl.BlockSpec(w_value.shape, lambda f: (0, 0)),
            pl.BlockSpec((1, count, channels), lambda f: (f, 0, 0)),
            pl.BlockSpec(w_output.shape, lambda f: (0, 0)),
        ],
        out_specs=pl.BlockSpec((1, count, channels), lambda f: (f, 0, 0)),
        out_shape=jax.ShapeDtypeStruct(queries.shape, queries.dtype),
        compiler_params=pltpu.CompilerParams(vmem_limit_bytes=60 * 1024 * 1024),
        cost_estimate=pl.CostEstimate(
            flops=flops, transcendentals=frames * count * tokens, bytes_accessed=moved
        ),
    )(queries, all_rows, w_key, w_value, residual, w_output)


def project_rows(tokens, weight):
    return jnp.einsum("ftc,cd->ftd", tokens, weight, preferred_element_type=jnp.float32).astype(
        jnp.bfloat16
    )


def per_device(
    features,
    first_cache,
    second_cache,
    w_query,
    w_key,
    w_value,
    w_output,
    w_first,
    w_upsample,
    w_second,
):
    frame_count, row_count, width_count, channels = features.shape
    core = lax.axis_index("ha") % 2
    count = lax.axis_size("ha")
    swap = [(i, i ^ 1) for i in range(count)]
    other = lax.dynamic_slice_in_dim(features, 1 - core, 1, axis=0)
    mine = lax.dynamic_slice_in_dim(features, core, 1, axis=0)
    block = jnp.concatenate([mine, lax.ppermute(other, "ha", swap)], axis=1)
    every_row = gather_chip_rows(block)
    all_rows = every_row.reshape(1, -1, channels)
    normed = rms_scale(block).astype(jnp.bfloat16)
    normed_tokens = normed.reshape(1, -1, channels)
    queries = project_rows(normed_tokens, w_query)
    score_scale = 1.0 / math.sqrt(channels)
    mixed_block = attend(
        queries,
        all_rows,
        w_key,
        w_value,
        block.reshape(queries.shape),
        w_output,
        score_scale,
    ).reshape(block.shape)
    back = lax.ppermute(mixed_block[:, 1:2], "ha", swap)
    own = mixed_block[:, 0:1]
    mixed = jnp.where(
        core == 0,
        jnp.concatenate([own, back], axis=0),
        jnp.concatenate([back, own], axis=0),
    )
    first_in = jax.nn.silu(rms_scale(mixed)).astype(jnp.bfloat16)
    first_stack = jnp.concatenate([first_cache, first_in], axis=0)
    first_padded = extended(first_stack, 1, 1)
    block_out = (mixed.astype(jnp.float32) + conv_taps(first_padded, w_first, 3)).astype(
        jnp.bfloat16
    )
    block_padded = extended(block_out, 1, 1)
    widened = jnp.repeat(block_padded, 2, axis=2)
    upsampled = conv_taps(widened, w_upsample[None], 1, rows=((0, 1), (1, 1), (1, 2))).astype(
        jnp.bfloat16
    )
    second_in = jax.nn.silu(rms_scale(upsampled)).astype(jnp.bfloat16)
    second_stack = jnp.concatenate([second_cache, second_in], axis=0)
    second_padded = extended(second_stack, 1, 1)
    return (upsampled.astype(jnp.float32) + conv_taps(second_padded, w_second, 3)).astype(
        jnp.bfloat16
    )


def solution(mesh):
    placed = (
        P("grp", "ha", None, None),
        P("grp", "ha", None, None),
        P("grp", "ha", None, None),
        P(),
        P(),
        P(),
        P(),
        P(),
        P(),
        P(),
    )
    return jax.shard_map(
        per_device,
        mesh=mesh,
        in_specs=placed,
        out_specs=P("grp", "ha", None, None),
        check_vma=False,
    )
```

```python
import functools
import math

import jax
import jax.numpy as jnp
from jax import lax
from jax.experimental import pallas as pl
from jax.experimental.pallas import tpu as pltpu
from jax.sharding import PartitionSpec as P


def halo_rows(x, dim, width):
    count, length = (lax.axis_size("ha"), x.shape[dim])
    up = [(i, i + 1) for i in range(count - 1)]
    down = [(j, i) for i, j in up]
    last = lax.slice_in_dim(x, length - width, length, axis=dim)
    first = lax.slice_in_dim(x, 0, width, axis=dim)
    before = lax.ppermute(last, "ha", up)
    after = lax.ppermute(first, "ha", down)
    return before, after


def extended(x, dim, width):
    before, after = halo_rows(x, dim, width)
    return jnp.concatenate([before, x, after], axis=dim)


def gather_chip_rows(x):
    count = lax.axis_size("ha")
    chips = count // 2
    ring = list(range(0, chips, 2)) + list(range(chips - 1 - chips % 2, 0, -2))
    if chips % 2:
        ring = list(range(chips))
    place = {c: i for i, c in enumerate(ring)}

    def toward(step):
        return [
            (2 * c + k, 2 * ring[(place[c] + step) % chips] + k)
            for c in range(chips)
            for k in range(2)
        ]

    forward, backward = toward(1), toward(-1)
    pieces = [x]
    ahead = behind = x
    for step in range(1, chips // 2 + 1):
        if step == chips - step and x.shape[1] > 1:
            half = x.shape[1] // 2
            first = lax.ppermute(ahead[:, :half], "ha", forward)
            second = lax.ppermute(behind[:, half:], "ha", backward)
            pieces.append(jnp.concatenate([first, second], axis=1))
            continue
        ahead = lax.ppermute(ahead, "ha", forward)
        pieces.append(ahead)
        if step < chips - step:
            behind = lax.ppermute(behind, "ha", backward)
            pieces.append(behind)
    return jnp.concatenate(pieces, axis=1)


def gather_rows(x):
    count = lax.axis_size("ha")
    chips = count // 2
    pieces = [x]
    for shift in range(1, chips):
        pairs = [
            (2 * c + k, 2 * ((c + shift) % chips) + k) for c in range(chips) for k in range(2)
        ]
        pieces.append(lax.ppermute(x, "ha", pairs))
    own_chip = jnp.concatenate(pieces, axis=1)
    swap = [(2 * c + k, 2 * c + 1 - k) for c in range(chips) for k in range(2)]
    other = lax.ppermute(own_chip, "ha", swap)
    return jnp.concatenate([own_chip, other], axis=1)


def rms_scale(tensor):
    widened = tensor.astype(jnp.float32)
    return widened * lax.rsqrt(jnp.mean(widened * widened, axis=-1, keepdims=True) + 1e-06)


def conv_taps(padded, weight, time_taps, rows=None):
    frames_out = padded.shape[0] - time_taps + 1
    height_out = padded.shape[1] - 2 if rows is None else len(rows[0])
    width_out = padded.shape[2]
    in_channels = weight.shape[-2]
    out_channels = weight.shape[-1]
    widened = jnp.pad(padded, ((0, 0), (0, 0), (1, 1), (0, 0)))
    result = jnp.zeros((frames_out, height_out, width_out, out_channels), jnp.float32)
    for time_off in range(time_taps):
        for row_off in range(3):
            if rows is None:
                window = widened[time_off : time_off + frames_out, row_off : row_off + height_out]
            else:
                window = jnp.stack(
                    [widened[time_off : time_off + frames_out, r] for r in rows[row_off]], axis=1
                )
            stacked = jnp.concatenate(
                [window[:, :, col_off : col_off + width_out] for col_off in range(3)], axis=-1
            )
            kernel = weight[time_off, row_off].reshape(3 * in_channels, out_channels)
            result = result + jnp.einsum(
                "fhwc,cd->fhwd", stacked, kernel, preferred_element_type=jnp.float32
            )
    return result


def attention_kernel(scale, q_ref, x_ref, wk_ref, wv_ref, r_ref, wo_ref, o_ref):
    raw = x_ref[0].astype(jnp.float32)
    tokens = (raw * lax.rsqrt(jnp.mean(raw * raw, axis=-1, keepdims=True) + 1e-06)).astype(
        x_ref.dtype
    )
    keys = jnp.dot(tokens, wk_ref[...], preferred_element_type=jnp.float32).astype(tokens.dtype)
    values = jnp.dot(tokens, wv_ref[...], preferred_element_type=jnp.float32).astype(tokens.dtype)
    scores = (
        lax.dot_general(
            q_ref[0], keys, (((1,), (1,)), ((), ())), preferred_element_type=jnp.float32
        )
        * scale
    )
    largest = jnp.max(scores, axis=-1, keepdims=True)
    weights = jnp.exp(scores - largest)
    weight_sum = jnp.sum(weights, axis=-1, keepdims=True)
    summed = jnp.dot(weights.astype(values.dtype), values, preferred_element_type=jnp.float32)
    attended = (summed / weight_sum).astype(values.dtype)
    projected = jnp.dot(attended, wo_ref[...], preferred_element_type=jnp.float32)
    o_ref[0] = (r_ref[0].astype(jnp.float32) + projected).astype(o_ref.dtype)


def attend(queries, all_rows, w_key, w_value, residual, w_output, scale):
    frames, count, channels = queries.shape
    tokens = all_rows.shape[1]
    flops = 4 * frames * count * tokens * channels + 4 * frames * tokens * channels * channels
    moved = 2 * (queries.size * 3 + all_rows.size + 3 * w_key.size)
    return pl.pallas_call(
        functools.partial(attention_kernel, scale),
        grid=(frames,),
        in_specs=[
            pl.BlockSpec((1, count, channels), lambda f: (f, 0, 0)),
            pl.BlockSpec((1, tokens, channels), lambda f: (f, 0, 0)),
            pl.BlockSpec(w_key.shape, lambda f: (0, 0)),
            pl.BlockSpec(w_value.shape, lambda f: (0, 0)),
            pl.BlockSpec((1, count, channels), lambda f: (f, 0, 0)),
            pl.BlockSpec(w_output.shape, lambda f: (0, 0)),
        ],
        out_specs=pl.BlockSpec((1, count, channels), lambda f: (f, 0, 0)),
        out_shape=jax.ShapeDtypeStruct(queries.shape, queries.dtype),
        compiler_params=pltpu.CompilerParams(vmem_limit_bytes=60 * 1024 * 1024),
        cost_estimate=pl.CostEstimate(
            flops=flops, transcendentals=frames * count * tokens, bytes_accessed=moved
        ),
    )(queries, all_rows, w_key, w_value, residual, w_output)


def project_rows(tokens, weight):
    return jnp.einsum("ftc,cd->ftd", tokens, weight, preferred_element_type=jnp.float32).astype(
        jnp.bfloat16
    )


def per_device(
    features,
    first_cache,
    second_cache,
    w_query,
    w_key,
    w_value,
    w_output,
    w_first,
    w_upsample,
    w_second,
):
    frame_count, row_count, width_count, channels = features.shape
    core = lax.axis_index("ha") % 2
    count = lax.axis_size("ha")
    swap = [(i, i ^ 1) for i in range(count)]
    partner = lax.ppermute(features, "ha", swap)
    mine = lax.dynamic_slice_in_dim(features, core, 1, axis=0)
    theirs = lax.dynamic_slice_in_dim(partner, core, 1, axis=0)
    block = jnp.concatenate([mine, theirs], axis=1)
    every_row = gather_chip_rows(block)
    all_rows = every_row.reshape(1, -1, channels)
    normed = rms_scale(block).astype(jnp.bfloat16)
    normed_tokens = normed.reshape(1, -1, channels)
    queries = project_rows(normed_tokens, w_query)
    score_scale = 1.0 / math.sqrt(channels)
    mixed_block = attend(
        queries,
        all_rows,
        w_key,
        w_value,
        block.reshape(queries.shape),
        w_output,
        score_scale,
    ).reshape(block.shape)
    back = lax.ppermute(mixed_block[:, 1:2], "ha", swap)
    own = mixed_block[:, 0:1]
    mixed = jnp.where(
        core == 0,
        jnp.concatenate([own, back], axis=0),
        jnp.concatenate([back, own], axis=0),
    )
    first_in = jax.nn.silu(rms_scale(mixed)).astype(jnp.bfloat16)
    first_stack = jnp.concatenate([first_cache, first_in], axis=0)
    first_padded = extended(first_stack, 1, 1)
    block_out = (mixed.astype(jnp.float32) + conv_taps(first_padded, w_first, 3)).astype(
        jnp.bfloat16
    )
    block_padded = extended(block_out, 1, 1)
    widened = jnp.repeat(block_padded, 2, axis=2)
    upsampled = conv_taps(widened, w_upsample[None], 1, rows=((0, 1), (1, 1), (1, 2))).astype(
        jnp.bfloat16
    )
    second_in = jax.nn.silu(rms_scale(upsampled)).astype(jnp.bfloat16)
    second_stack = jnp.concatenate([second_cache, second_in], axis=0)
    second_padded = extended(second_stack, 1, 1)
    return (upsampled.astype(jnp.float32) + conv_taps(second_padded, w_second, 3)).astype(
        jnp.bfloat16
    )


def solution(mesh):
    placed = (
        P("grp", "ha", None, None),
        P("grp", "ha", None, None),
        P("grp", "ha", None, None),
        P(),
        P(),
        P(),
        P(),
        P(),
        P(),
        P(),
    )
    return jax.shard_map(
        per_device,
        mesh=mesh,
        in_specs=placed,
        out_specs=P("grp", "ha", None, None),
        check_vma=False,
    )
```

```python
import functools
import math

import jax
import jax.numpy as jnp
from jax import lax
from jax.experimental import pallas as pl
from jax.experimental.pallas import tpu as pltpu
from jax.sharding import PartitionSpec as P


def halo_rows(x, dim, width):
    count, length = (lax.axis_size("ha"), x.shape[dim])
    up = [(i, i + 1) for i in range(count - 1)]
    down = [(j, i) for i, j in up]
    last = lax.slice_in_dim(x, length - width, length, axis=dim)
    first = lax.slice_in_dim(x, 0, width, axis=dim)
    before = lax.ppermute(last, "ha", up)
    after = lax.ppermute(first, "ha", down)
    return before, after


def extended(x, dim, width):
    before, after = halo_rows(x, dim, width)
    return jnp.concatenate([before, x, after], axis=dim)


def gather_chip_rows(x):
    count = lax.axis_size("ha")
    chips = count // 2
    ring = list(range(0, chips, 2)) + list(range(chips - 1 - chips % 2, 0, -2))
    if chips % 2:
        ring = list(range(chips))
    place = {c: i for i, c in enumerate(ring)}

    def toward(step):
        return [
            (2 * c + k, 2 * ring[(place[c] + step) % chips] + k)
            for c in range(chips)
            for k in range(2)
        ]

    forward, backward = toward(1), toward(-1)
    pieces = [x]
    ahead = behind = x
    for step in range(1, chips // 2 + 1):
        if step == chips - step and x.shape[1] > 1:
            half = x.shape[1] // 2
            first = lax.ppermute(ahead[:, :half], "ha", forward)
            second = lax.ppermute(behind[:, half:], "ha", backward)
            pieces.append(jnp.concatenate([first, second], axis=1))
            continue
        ahead = lax.ppermute(ahead, "ha", forward)
        pieces.append(ahead)
        if step < chips - step:
            behind = lax.ppermute(behind, "ha", backward)
            pieces.append(behind)
    return jnp.concatenate(pieces, axis=1)


def gather_rows(x):
    count = lax.axis_size("ha")
    chips = count // 2
    pieces = [x]
    for shift in range(1, chips):
        pairs = [
            (2 * c + k, 2 * ((c + shift) % chips) + k) for c in range(chips) for k in range(2)
        ]
        pieces.append(lax.ppermute(x, "ha", pairs))
    own_chip = jnp.concatenate(pieces, axis=1)
    swap = [(2 * c + k, 2 * c + 1 - k) for c in range(chips) for k in range(2)]
    other = lax.ppermute(own_chip, "ha", swap)
    return jnp.concatenate([own_chip, other], axis=1)


def rms_scale(tensor):
    widened = tensor.astype(jnp.float32)
    return widened * lax.rsqrt(jnp.mean(widened * widened, axis=-1, keepdims=True) + 1e-06)


def conv_pieces(x, weight, time_taps):
    before, after = halo_rows(x, 1, 1)
    pieces = [before] + [x[:, i : i + 1] for i in range(x.shape[1])] + [after]
    frames_out = x.shape[0] - time_taps + 1
    height_out = x.shape[1]
    width_out = x.shape[2]
    in_channels = weight.shape[-2]
    result = None
    for time_off in range(time_taps):
        for row_off in range(3):
            window = jnp.concatenate(
                [p[time_off : time_off + frames_out] for p in pieces[row_off : row_off + height_out]],
                axis=1,
            )
            window = jnp.pad(window, ((0, 0), (0, 0), (1, 1), (0, 0)))
            stacked = jnp.concatenate(
                [window[:, :, col_off : col_off + width_out] for col_off in range(3)], axis=-1
            )
            kernel = weight[time_off, row_off].reshape(3 * in_channels, weight.shape[-1])
            term = jnp.einsum("fhwc,cd->fhwd", stacked, kernel, preferred_element_type=jnp.float32)
            result = term if result is None else result + term
    return result


def conv_taps(padded, weight, time_taps, rows=None):
    frames_out = padded.shape[0] - time_taps + 1
    height_out = padded.shape[1] - 2 if rows is None else len(rows[0])
    width_out = padded.shape[2]
    in_channels = weight.shape[-2]
    out_channels = weight.shape[-1]
    widened = jnp.pad(padded, ((0, 0), (0, 0), (1, 1), (0, 0)))
    result = jnp.zeros((frames_out, height_out, width_out, out_channels), jnp.float32)
    for time_off in range(time_taps):
        for row_off in range(3):
            if rows is None:
                window = widened[time_off : time_off + frames_out, row_off : row_off + height_out]
            else:
                window = jnp.stack(
                    [widened[time_off : time_off + frames_out, r] for r in rows[row_off]], axis=1
                )
            stacked = jnp.concatenate(
                [window[:, :, col_off : col_off + width_out] for col_off in range(3)], axis=-1
            )
            kernel = weight[time_off, row_off].reshape(3 * in_channels, out_channels)
            result = result + jnp.einsum(
                "fhwc,cd->fhwd", stacked, kernel, preferred_element_type=jnp.float32
            )
    return result


def attention_kernel(scale, q_ref, x_ref, wk_ref, wv_ref, r_ref, wo_ref, o_ref):
    raw = x_ref[0].astype(jnp.float32)
    tokens = (raw * lax.rsqrt(jnp.mean(raw * raw, axis=-1, keepdims=True) + 1e-06)).astype(
        x_ref.dtype
    )
    keys = jnp.dot(tokens, wk_ref[...], preferred_element_type=jnp.float32).astype(tokens.dtype)
    values = jnp.dot(tokens, wv_ref[...], preferred_element_type=jnp.float32).astype(tokens.dtype)
    scores = (
        lax.dot_general(
            q_ref[0], keys, (((1,), (1,)), ((), ())), preferred_element_type=jnp.float32
        )
        * scale
    )
    largest = jnp.max(scores, axis=-1, keepdims=True)
    weights = jnp.exp(scores - largest)
    weight_sum = jnp.sum(weights, axis=-1, keepdims=True)
    summed = jnp.dot(weights.astype(values.dtype), values, preferred_element_type=jnp.float32)
    attended = (summed / weight_sum).astype(values.dtype)
    projected = jnp.dot(attended, wo_ref[...], preferred_element_type=jnp.float32)
    o_ref[0] = (r_ref[0].astype(jnp.float32) + projected).astype(o_ref.dtype)


def attend(queries, all_rows, w_key, w_value, residual, w_output, scale):
    frames, count, channels = queries.shape
    tokens = all_rows.shape[1]
    flops = 4 * frames * count * tokens * channels + 4 * frames * tokens * channels * channels
    moved = 2 * (queries.size * 3 + all_rows.size + 3 * w_key.size)
    return pl.pallas_call(
        functools.partial(attention_kernel, scale),
        grid=(frames,),
        in_specs=[
            pl.BlockSpec((1, count, channels), lambda f: (f, 0, 0)),
            pl.BlockSpec((1, tokens, channels), lambda f: (f, 0, 0)),
            pl.BlockSpec(w_key.shape, lambda f: (0, 0)),
            pl.BlockSpec(w_value.shape, lambda f: (0, 0)),
            pl.BlockSpec((1, count, channels), lambda f: (f, 0, 0)),
            pl.BlockSpec(w_output.shape, lambda f: (0, 0)),
        ],
        out_specs=pl.BlockSpec((1, count, channels), lambda f: (f, 0, 0)),
        out_shape=jax.ShapeDtypeStruct(queries.shape, queries.dtype),
        compiler_params=pltpu.CompilerParams(vmem_limit_bytes=60 * 1024 * 1024),
        cost_estimate=pl.CostEstimate(
            flops=flops, transcendentals=frames * count * tokens, bytes_accessed=moved
        ),
    )(queries, all_rows, w_key, w_value, residual, w_output)


def project_rows(tokens, weight):
    return jnp.einsum("ftc,cd->ftd", tokens, weight, preferred_element_type=jnp.float32).astype(
        jnp.bfloat16
    )


def per_device(
    features,
    first_cache,
    second_cache,
    w_query,
    w_key,
    w_value,
    w_output,
    w_first,
    w_upsample,
    w_second,
):
    frame_count, row_count, width_count, channels = features.shape
    core = lax.axis_index("ha") % 2
    count = lax.axis_size("ha")
    swap = [(i, i ^ 1) for i in range(count)]
    partner = lax.ppermute(features, "ha", swap)
    mine = lax.dynamic_slice_in_dim(features, core, 1, axis=0)
    theirs = lax.dynamic_slice_in_dim(partner, core, 1, axis=0)
    block = jnp.concatenate([mine, theirs], axis=1)
    every_row = gather_chip_rows(block)
    all_rows = every_row.reshape(1, -1, channels)
    normed = rms_scale(block).astype(jnp.bfloat16)
    normed_tokens = normed.reshape(1, -1, channels)
    queries = project_rows(normed_tokens, w_query)
    score_scale = 1.0 / math.sqrt(channels)
    mixed_block = attend(
        queries,
        all_rows,
        w_key,
        w_value,
        block.reshape(queries.shape),
        w_output,
        score_scale,
    ).reshape(block.shape)
    back = lax.ppermute(mixed_block[:, 1:2], "ha", swap)
    own = mixed_block[:, 0:1]
    mixed = jnp.where(
        core == 0,
        jnp.concatenate([own, back], axis=0),
        jnp.concatenate([back, own], axis=0),
    )
    first_in = jax.nn.silu(rms_scale(mixed)).astype(jnp.bfloat16)
    first_stack = jnp.concatenate([first_cache, first_in], axis=0)
    block_out = (mixed.astype(jnp.float32) + conv_pieces(first_stack, w_first, 3)).astype(
        jnp.bfloat16
    )
    block_padded = extended(block_out, 1, 1)
    widened = jnp.repeat(block_padded, 2, axis=2)
    upsampled = conv_taps(widened, w_upsample[None], 1, rows=((0, 1), (1, 1), (1, 2))).astype(
        jnp.bfloat16
    )
    second_in = jax.nn.silu(rms_scale(upsampled)).astype(jnp.bfloat16)
    second_stack = jnp.concatenate([second_cache, second_in], axis=0)
    return (upsampled.astype(jnp.float32) + conv_pieces(second_stack, w_second, 3)).astype(
        jnp.bfloat16
    )


def solution(mesh):
    placed = (
        P("grp", "ha", None, None),
        P("grp", "ha", None, None),
        P("grp", "ha", None, None),
        P(),
        P(),
        P(),
        P(),
        P(),
        P(),
        P(),
    )
    return jax.shard_map(
        per_device,
        mesh=mesh,
        in_specs=placed,
        out_specs=P("grp", "ha", None, None),
        check_vma=False,
    )
```

```python
import functools
import math

import jax
import jax.numpy as jnp
from jax import lax
from jax.experimental import pallas as pl
from jax.experimental.pallas import tpu as pltpu
from jax.sharding import PartitionSpec as P


def halo_rows(x, dim, width):
    count, length = (lax.axis_size("ha"), x.shape[dim])
    up = [(i, i + 1) for i in range(count - 1)]
    down = [(j, i) for i, j in up]
    last = lax.slice_in_dim(x, length - width, length, axis=dim)
    first = lax.slice_in_dim(x, 0, width, axis=dim)
    before = lax.ppermute(last, "ha", up)
    after = lax.ppermute(first, "ha", down)
    return before, after


def extended(x, dim, width):
    before, after = halo_rows(x, dim, width)
    return jnp.concatenate([before, x, after], axis=dim)


def gather_chip_rows(x):
    count = lax.axis_size("ha")
    chips = count // 2
    ring = list(range(0, chips, 2)) + list(range(chips - 1 - chips % 2, 0, -2))
    if chips % 2:
        ring = list(range(chips))
    place = {c: i for i, c in enumerate(ring)}

    def toward(step):
        return [
            (2 * c + k, 2 * ring[(place[c] + step) % chips] + k)
            for c in range(chips)
            for k in range(2)
        ]

    forward, backward = toward(1), toward(-1)
    pieces = [x]
    ahead = behind = x
    for step in range(1, chips // 2 + 1):
        if step == chips - step and x.shape[1] > 1:
            half = x.shape[1] // 2
            first = lax.ppermute(ahead[:, :half], "ha", forward)
            second = lax.ppermute(behind[:, half:], "ha", backward)
            pieces.append(jnp.concatenate([first, second], axis=1))
            continue
        ahead = lax.ppermute(ahead, "ha", forward)
        pieces.append(ahead)
        if step < chips - step:
            behind = lax.ppermute(behind, "ha", backward)
            pieces.append(behind)
    return jnp.concatenate(pieces, axis=1)


def gather_rows(x):
    count = lax.axis_size("ha")
    chips = count // 2
    pieces = [x]
    for shift in range(1, chips):
        pairs = [
            (2 * c + k, 2 * ((c + shift) % chips) + k) for c in range(chips) for k in range(2)
        ]
        pieces.append(lax.ppermute(x, "ha", pairs))
    own_chip = jnp.concatenate(pieces, axis=1)
    swap = [(2 * c + k, 2 * c + 1 - k) for c in range(chips) for k in range(2)]
    other = lax.ppermute(own_chip, "ha", swap)
    return jnp.concatenate([own_chip, other], axis=1)


def rms_scale(tensor):
    widened = tensor.astype(jnp.float32)
    return widened * lax.rsqrt(jnp.mean(widened * widened, axis=-1, keepdims=True) + 1e-06)


def conv_taps(padded, weight, time_taps, rows=None):
    frames_out = padded.shape[0] - time_taps + 1
    height_out = padded.shape[1] - 2 if rows is None else len(rows[0])
    width_out = padded.shape[2]
    in_channels = weight.shape[-2]
    out_channels = weight.shape[-1]
    widened = jnp.pad(padded, ((0, 0), (0, 0), (1, 1), (0, 0)))
    result = jnp.zeros((frames_out, height_out, width_out, out_channels), jnp.float32)
    for time_off in range(time_taps):
        for row_off in range(3):
            if rows is None:
                window = widened[time_off : time_off + frames_out, row_off : row_off + height_out]
            else:
                window = jnp.stack(
                    [widened[time_off : time_off + frames_out, r] for r in rows[row_off]], axis=1
                )
            stacked = jnp.concatenate(
                [window[:, :, col_off : col_off + width_out] for col_off in range(3)], axis=-1
            )
            kernel = weight[time_off, row_off].reshape(3 * in_channels, out_channels)
            result = result + jnp.einsum(
                "fhwc,cd->fhwd", stacked, kernel, preferred_element_type=jnp.float32
            )
    return result


def attention_kernel(scale, q_ref, x_ref, wk_ref, wv_ref, r_ref, wo_ref, own_ref, other_ref):
    raw = x_ref[0].astype(jnp.float32)
    tokens = (raw * lax.rsqrt(jnp.mean(raw * raw, axis=-1, keepdims=True) + 1e-06)).astype(
        x_ref.dtype
    )
    keys = jnp.dot(tokens, wk_ref[...], preferred_element_type=jnp.float32).astype(tokens.dtype)
    values = jnp.dot(tokens, wv_ref[...], preferred_element_type=jnp.float32).astype(tokens.dtype)
    scores = (
        lax.dot_general(
            q_ref[0], keys, (((1,), (1,)), ((), ())), preferred_element_type=jnp.float32
        )
        * scale
    )
    largest = jnp.max(scores, axis=-1, keepdims=True)
    weights = jnp.exp(scores - largest)
    weight_sum = jnp.sum(weights, axis=-1, keepdims=True)
    summed = jnp.dot(weights.astype(values.dtype), values, preferred_element_type=jnp.float32)
    attended = (summed / weight_sum).astype(values.dtype)
    projected = jnp.dot(attended, wo_ref[...], preferred_element_type=jnp.float32)
    mixed = (r_ref[0].astype(jnp.float32) + projected).astype(own_ref.dtype)
    half = own_ref.shape[1]
    own_ref[0] = mixed[:half]
    other_ref[0] = mixed[half:]


def attend(queries, all_rows, w_key, w_value, residual, w_output, scale):
    frames, count, channels = queries.shape
    tokens = all_rows.shape[1]
    flops = 4 * frames * count * tokens * channels + 4 * frames * tokens * channels * channels
    moved = 2 * (queries.size * 3 + all_rows.size + 3 * w_key.size)
    return pl.pallas_call(
        functools.partial(attention_kernel, scale),
        grid=(frames,),
        in_specs=[
            pl.BlockSpec((1, count, channels), lambda f: (f, 0, 0)),
            pl.BlockSpec((1, tokens, channels), lambda f: (f, 0, 0)),
            pl.BlockSpec(w_key.shape, lambda f: (0, 0)),
            pl.BlockSpec(w_value.shape, lambda f: (0, 0)),
            pl.BlockSpec((1, count, channels), lambda f: (f, 0, 0)),
            pl.BlockSpec(w_output.shape, lambda f: (0, 0)),
        ],
        out_specs=[pl.BlockSpec((1, count // 2, channels), lambda f: (f, 0, 0))] * 2,
        out_shape=[jax.ShapeDtypeStruct((frames, count // 2, channels), queries.dtype)] * 2,
        compiler_params=pltpu.CompilerParams(vmem_limit_bytes=60 * 1024 * 1024),
        cost_estimate=pl.CostEstimate(
            flops=flops, transcendentals=frames * count * tokens, bytes_accessed=moved
        ),
    )(queries, all_rows, w_key, w_value, residual, w_output)


def project_rows(tokens, weight):
    return jnp.einsum("ftc,cd->ftd", tokens, weight, preferred_element_type=jnp.float32).astype(
        jnp.bfloat16
    )


def per_device(
    features,
    first_cache,
    second_cache,
    w_query,
    w_key,
    w_value,
    w_output,
    w_first,
    w_upsample,
    w_second,
):
    frame_count, row_count, width_count, channels = features.shape
    core = lax.axis_index("ha") % 2
    count = lax.axis_size("ha")
    swap = [(i, i ^ 1) for i in range(count)]
    partner = lax.ppermute(features, "ha", swap)
    mine = lax.dynamic_slice_in_dim(features, core, 1, axis=0)
    theirs = lax.dynamic_slice_in_dim(partner, core, 1, axis=0)
    block = jnp.concatenate([mine, theirs], axis=1)
    every_row = gather_chip_rows(block)
    all_rows = every_row.reshape(1, -1, channels)
    normed = rms_scale(block).astype(jnp.bfloat16)
    normed_tokens = normed.reshape(1, -1, channels)
    queries = project_rows(normed_tokens, w_query)
    score_scale = 1.0 / math.sqrt(channels)
    own, theirs = attend(
        queries,
        all_rows,
        w_key,
        w_value,
        block.reshape(queries.shape),
        w_output,
        score_scale,
    )
    row_shape = mine.shape
    back = lax.ppermute(theirs.reshape(row_shape), "ha", swap)
    own = own.reshape(row_shape)
    mixed = jnp.where(
        core == 0,
        jnp.concatenate([own, back], axis=0),
        jnp.concatenate([back, own], axis=0),
    )
    first_in = jax.nn.silu(rms_scale(mixed)).astype(jnp.bfloat16)
    first_stack = jnp.concatenate([first_cache, first_in], axis=0)
    first_padded = extended(first_stack, 1, 1)
    block_out = (mixed.astype(jnp.float32) + conv_taps(first_padded, w_first, 3)).astype(
        jnp.bfloat16
    )
    block_padded = extended(block_out, 1, 1)
    widened = jnp.repeat(block_padded, 2, axis=2)
    upsampled = conv_taps(widened, w_upsample[None], 1, rows=((0, 1), (1, 1), (1, 2))).astype(
        jnp.bfloat16
    )
    second_in = jax.nn.silu(rms_scale(upsampled)).astype(jnp.bfloat16)
    second_stack = jnp.concatenate([second_cache, second_in], axis=0)
    second_padded = extended(second_stack, 1, 1)
    return (upsampled.astype(jnp.float32) + conv_taps(second_padded, w_second, 3)).astype(
        jnp.bfloat16
    )


def solution(mesh):
    placed = (
        P("grp", "ha", None, None),
        P("grp", "ha", None, None),
        P("grp", "ha", None, None),
        P(),
        P(),
        P(),
        P(),
        P(),
        P(),
        P(),
    )
    return jax.shard_map(
        per_device,
        mesh=mesh,
        in_specs=placed,
        out_specs=P("grp", "ha", None, None),
        check_vma=False,
    )
```

```python
import functools
import math

import jax
import jax.numpy as jnp
from jax import lax
from jax.experimental import pallas as pl
from jax.experimental.pallas import tpu as pltpu
from jax.sharding import PartitionSpec as P


def halo_rows(x, dim, width):
    count, length = (lax.axis_size("ha"), x.shape[dim])
    up = [(i, i + 1) for i in range(count - 1)]
    down = [(j, i) for i, j in up]
    last = lax.slice_in_dim(x, length - width, length, axis=dim)
    first = lax.slice_in_dim(x, 0, width, axis=dim)
    before = lax.ppermute(last, "ha", up)
    after = lax.ppermute(first, "ha", down)
    return before, after


def extended(x, dim, width):
    before, after = halo_rows(x, dim, width)
    return jnp.concatenate([before, x, after], axis=dim)


def gather_chip_rows(x):
    count = lax.axis_size("ha")
    chips = count // 2
    ring = list(range(0, chips, 2)) + list(range(chips - 1 - chips % 2, 0, -2))
    if chips % 2:
        ring = list(range(chips))
    place = {c: i for i, c in enumerate(ring)}

    def toward(step):
        return [
            (2 * c + k, 2 * ring[(place[c] + step) % chips] + k)
            for c in range(chips)
            for k in range(2)
        ]

    forward, backward = toward(1), toward(-1)
    pieces = [x]
    ahead = behind = x
    for step in range(1, chips // 2 + 1):
        if step == chips - step and x.shape[1] > 1:
            half = x.shape[1] // 2
            first = lax.ppermute(ahead[:, :half], "ha", forward)
            second = lax.ppermute(behind[:, half:], "ha", backward)
            pieces.append(jnp.concatenate([first, second], axis=1))
            continue
        ahead = lax.ppermute(ahead, "ha", forward)
        pieces.append(ahead)
        if step < chips - step:
            behind = lax.ppermute(behind, "ha", backward)
            pieces.append(behind)
    return jnp.concatenate(pieces, axis=1)


def gather_rows(x):
    count = lax.axis_size("ha")
    chips = count // 2
    pieces = [x]
    for shift in range(1, chips):
        pairs = [
            (2 * c + k, 2 * ((c + shift) % chips) + k) for c in range(chips) for k in range(2)
        ]
        pieces.append(lax.ppermute(x, "ha", pairs))
    own_chip = jnp.concatenate(pieces, axis=1)
    swap = [(2 * c + k, 2 * c + 1 - k) for c in range(chips) for k in range(2)]
    other = lax.ppermute(own_chip, "ha", swap)
    return jnp.concatenate([own_chip, other], axis=1)


def rms_scale(tensor):
    widened = tensor.astype(jnp.float32)
    return widened * lax.rsqrt(jnp.mean(widened * widened, axis=-1, keepdims=True) + 1e-06)


def conv_taps(padded, weight, time_taps, rows=None):
    frames_out = padded.shape[0] - time_taps + 1
    height_out = padded.shape[1] - 2 if rows is None else len(rows[0])
    width_out = padded.shape[2]
    in_channels = weight.shape[-2]
    out_channels = weight.shape[-1]
    widened = jnp.pad(padded, ((0, 0), (0, 0), (1, 1), (0, 0)))
    result = jnp.zeros((frames_out, height_out, width_out, out_channels), jnp.float32)
    for time_off in range(time_taps):
        for row_off in range(3):
            if rows is None:
                window = widened[time_off : time_off + frames_out, row_off : row_off + height_out]
            else:
                window = jnp.stack(
                    [widened[time_off : time_off + frames_out, r] for r in rows[row_off]], axis=1
                )
            stacked = jnp.concatenate(
                [window[:, :, col_off : col_off + width_out] for col_off in range(3)], axis=-1
            )
            kernel = weight[time_off, row_off].reshape(3 * in_channels, out_channels)
            result = result + jnp.einsum(
                "fhwc,cd->fhwd", stacked, kernel, preferred_element_type=jnp.float32
            )
    return result


def attention_kernel(scale, q_ref, x_ref, wk_ref, wv_ref, r_ref, wo_ref, o_ref):
    raw = x_ref[0].astype(jnp.float32)
    tokens = (raw * lax.rsqrt(jnp.mean(raw * raw, axis=-1, keepdims=True) + 1e-06)).astype(
        x_ref.dtype
    )
    keys = jnp.dot(tokens, wk_ref[...], preferred_element_type=jnp.float32).astype(tokens.dtype)
    values = jnp.dot(tokens, wv_ref[...], preferred_element_type=jnp.float32).astype(tokens.dtype)
    scores = (
        lax.dot_general(
            q_ref[0], keys, (((1,), (1,)), ((), ())), preferred_element_type=jnp.float32
        )
        * scale
    )
    largest = jnp.max(scores, axis=-1, keepdims=True)
    weights = jnp.exp(scores - largest)
    weight_sum = jnp.sum(weights, axis=-1, keepdims=True)
    summed = jnp.dot(weights.astype(values.dtype), values, preferred_element_type=jnp.float32)
    attended = (summed / weight_sum).astype(values.dtype)
    projected = jnp.dot(attended, wo_ref[...], preferred_element_type=jnp.float32)
    o_ref[0] = (r_ref[0].astype(jnp.float32) + projected).astype(o_ref.dtype)


def attend(queries, all_rows, w_key, w_value, residual, w_output, scale):
    frames, count, channels = queries.shape
    tokens = all_rows.shape[1]
    flops = 4 * frames * count * tokens * channels + 4 * frames * tokens * channels * channels
    moved = 2 * (queries.size * 3 + all_rows.size + 3 * w_key.size)
    return pl.pallas_call(
        functools.partial(attention_kernel, scale),
        grid=(frames,),
        in_specs=[
            pl.BlockSpec((1, count, channels), lambda f: (f, 0, 0)),
            pl.BlockSpec((1, tokens, channels), lambda f: (f, 0, 0)),
            pl.BlockSpec(w_key.shape, lambda f: (0, 0)),
            pl.BlockSpec(w_value.shape, lambda f: (0, 0)),
            pl.BlockSpec((1, count, channels), lambda f: (f, 0, 0)),
            pl.BlockSpec(w_output.shape, lambda f: (0, 0)),
        ],
        out_specs=pl.BlockSpec((1, count, channels), lambda f: (f, 0, 0)),
        out_shape=jax.ShapeDtypeStruct(queries.shape, queries.dtype),
        compiler_params=pltpu.CompilerParams(vmem_limit_bytes=60 * 1024 * 1024),
        cost_estimate=pl.CostEstimate(
            flops=flops, transcendentals=frames * count * tokens, bytes_accessed=moved
        ),
    )(queries, all_rows, w_key, w_value, residual, w_output)


def project_rows(tokens, weight):
    return jnp.einsum("ftc,cd->ftd", tokens, weight, preferred_element_type=jnp.float32).astype(
        jnp.bfloat16
    )


def per_device(
    features,
    first_cache,
    second_cache,
    w_query,
    w_key,
    w_value,
    w_output,
    w_first,
    w_upsample,
    w_second,
):
    frame_count, row_count, width_count, channels = features.shape
    core = lax.axis_index("ha") % 2
    count = lax.axis_size("ha")
    swap = [(i, i ^ 1) for i in range(count)]
    partner = lax.ppermute(features, "ha", swap)
    mine = lax.dynamic_slice_in_dim(features, core, 1, axis=0)
    theirs = lax.dynamic_slice_in_dim(partner, core, 1, axis=0)
    block = jnp.concatenate([mine, theirs], axis=1)
    every_row = gather_chip_rows(block)
    all_rows = every_row.reshape(1, -1, channels)
    normed = rms_scale(block).astype(jnp.bfloat16)
    normed_tokens = normed.reshape(1, -1, channels)
    queries = project_rows(normed_tokens, w_query)
    score_scale = 1.0 / math.sqrt(channels)
    mixed_block = attend(
        queries,
        all_rows,
        w_key,
        w_value,
        block.reshape(queries.shape),
        w_output,
        score_scale,
    ).reshape(block.shape)
    back = lax.ppermute(mixed_block[:, 1:2], "ha", swap)
    own = mixed_block[:, 0:1]
    mixed = jnp.where(
        core == 0,
        jnp.concatenate([own, back], axis=0),
        jnp.concatenate([back, own], axis=0),
    )
    first_in = jax.nn.silu(rms_scale(mixed)).astype(jnp.bfloat16)
    first_stack = jnp.concatenate([first_cache, first_in], axis=0)
    first_padded = extended(first_stack, 1, 1)
    block_out = (mixed.astype(jnp.float32) + conv_taps(first_padded, w_first, 3)).astype(
        jnp.bfloat16
    )
    block_out, later_cache = lax.optimization_barrier((block_out, second_cache))
    cache_padded = extended(later_cache, 1, 1)
    block_padded = extended(block_out, 1, 1)
    widened = jnp.repeat(block_padded, 2, axis=2)
    upsampled = conv_taps(widened, w_upsample[None], 1, rows=((0, 1), (1, 1), (1, 2))).astype(
        jnp.bfloat16
    )
    second_in = jax.nn.silu(rms_scale(upsampled)).astype(jnp.bfloat16)
    second_padded = jnp.concatenate([cache_padded, extended(second_in, 1, 1)], axis=0)
    return (upsampled.astype(jnp.float32) + conv_taps(second_padded, w_second, 3)).astype(
        jnp.bfloat16
    )


def solution(mesh):
    placed = (
        P("grp", "ha", None, None),
        P("grp", "ha", None, None),
        P("grp", "ha", None, None),
        P(),
        P(),
        P(),
        P(),
        P(),
        P(),
        P(),
    )
    return jax.shard_map(
        per_device,
        mesh=mesh,
        in_specs=placed,
        out_specs=P("grp", "ha", None, None),
        check_vma=False,
    )
```
